128 devices in a mesh: req: 16 (over y, z), tp: 8 (over x, core).
Axes of the slice: x: 4, y: 4, z: 4, core: 2. Of those that a mesh axis runs over, the one named last changes fastest.
Arguments:
- suffix_tokens: bfloat16 [256, 112, 2880], P('req'), may hold values from -40 to 40
- route_lengths: int32 [16, 16], replicated, may hold values from 1 to 112, 768 in all within a row
- dest_perm: int32 [16, 16], replicated, may hold values from 0 to 15, each once within a row
- attach_points: int32 [256], replicated, may hold values from 256 to 8192
- prefix_cache: bfloat16 [64, 128, 8, 128], P('req', None, 'tp'), may hold values from -120 to 120
- block_of_slot: int32 [64], replicated, may hold values from 0 to 63, each once
- sink_logits: float32 [64], P('tp'), may hold values from 0 to 6
- attn_gain: bfloat16 [2880], replicated, may hold values from 0.099609375 to 1.8984375
- w_query: bfloat16 [2880, 4096], P(None, 'tp'), may hold values from -0.109375 to 0.109375
- w_keyval: bfloat16 [2880, 8, 128], P(None, 'tp'), may hold values from -0.109375 to 0.109375
- w_out: bfloat16 [4096, 2880], P('tp'), may hold values from -0.09375 to 0.09375
- mlp_gain: bfloat16 [2880], replicated, may hold values from 0.099609375 to 1.8984375
- w_gate: bfloat16 [2880, 2880], P(None, 'tp'), may hold values from -0.109375 to 0.109375
- w_up: bfloat16 [2880, 2880], P(None, 'tp'), may hold values from -0.109375 to 0.109375
- w_down: bfloat16 [2880, 2880], P('tp'), may hold values from -0.109375 to 0.109375
Outputs:
- layer_out: bfloat16 [256, 112, 2880], P('req', None, 'tp')
The draws below stay inside these ranges and needn't reach their ends.
Inputs may be any that keep to these rules, and one draw needn't show every extreme that they name: `route_lengths`: each row sums to 768, and the largest entry of each row is 112. `dest_perm`: each row is a permutation of the devices of req. `block_of_slot`: a permutation.
All inputs are finite; a program needn't handle non-finite values.
Results may differ from the reference program's by a relative error of at most 0.013.
Values may be sent and summed in bfloat16 or wider, within the bound.
No kernel may reach another device: no remote copies, remote signals or barrier semaphores. Data moves between devices by JAX's collectives and lax.ppermute only.
A program may use at most 192 MiB of HBM per device.

```python
import math
import jax
import jax.numpy as jnp
import numpy as np
from jax import lax

D = 2880
HQ = 64
KVH = 8
HD = 64
FF = 2880
WINDOW = 128
PREFIX = 8192
PBLK = 128
MAXLEN = 112
CAP = 768
REQUESTS = 256
PBLOCKS = 64
N_REQ = 16
N_TP = 8


def draw_suffix_tokens(key, part):
    column_key, row_key, base_key = jax.random.split(key, 3)
    full_shape = (REQUESTS, MAXLEN, D)
    position_ramp = jnp.arange(D).astype(jnp.float32) / (D - 1)
    columns = jnp.exp(math.log(3.0) * (position_ramp - 0.5)) * jax.random.uniform(column_key, (D,), minval=0.7, maxval=1.3)
    row_scale = jnp.exp(jax.random.uniform(row_key, (REQUESTS, MAXLEN, 1), minval=math.log(0.3), maxval=math.log(3.0)))
    base_values = jax.random.normal(base_key, full_shape)
    return jnp.clip(base_values * row_scale * columns, -40.0, 40.0).astype(jnp.bfloat16)


def draw_prefix_cache(key, part):
    value_key, boost_key = jax.random.split(key, 2)
    full_shape = (PBLOCKS, PBLK, KVH, 2 * HD)
    base_values = jax.random.normal(value_key, full_shape)
    row_boost = jnp.exp(jax.random.uniform(boost_key, (PBLOCKS, PBLK, KVH, 1), minval=math.log(0.5), maxval=math.log(2.0)))
    key_lanes = jnp.arange(2 * HD) < HD
    return jnp.clip(jnp.where(key_lanes, base_values * row_boost, base_values), -120.0, 120.0).astype(jnp.bfloat16)


def set_ends(drawn, stream_key, least, top_value):
    extent = drawn.shape
    spot = [jax.random.randint(jax.random.fold_in(stream_key, axis), (), 0, extent[axis]) for axis in range(len(extent))]
    drawn = drawn.at[tuple(spot)].set(least)
    longest = extent.index(max(extent))
    spot[longest] = (spot[longest] + 1) % extent[longest]
    return drawn.at[tuple(spot)].set(top_value)


def steps_of(own_key, shape, cuts, least, top_value):
    level, own = 1.0, jax.random.fold_in(own_key, 6)
    for axis_at, shards_of in cuts:
        draws = jnp.exp(jax.random.uniform(jax.random.fold_in(own, axis_at), (shards_of,), jnp.float32, least / len(cuts), top_value / len(cuts)))
        level = level * jnp.repeat(draws, shape[axis_at] // shards_of).reshape([-1 if axis == axis_at else 1 for axis in range(len(shape))])
    return level


def profile(number_of, total, bound, slope):
    portions = [(1 << 20) // math.isqrt(standing ** slope) + 1 for standing in range(2, number_of + 1)]
    surplus, counts = total - bound - (number_of - 1), [1] * (number_of - 1)
    while surplus > 0:
        free = [i for i in range(number_of - 1) if counts[i] < bound]
        whole, left = sum([portions[i] for i in free]), surplus
        for i in free:
            more = min(bound - counts[i], max(1, left * portions[i] // whole), surplus)
            counts[i] = counts[i] + more
            surplus = surplus - more
    return np.array([bound] + counts)


def uneven(own_key, amount, total, reach, lean):
    if amount == 2:
        one = jax.random.randint(own_key, (), max(1, total - reach), min(reach, total - 1) + 1)
        return jnp.stack([one, total - one])
    sizes = jnp.asarray(profile(amount, total, reach, lean), jnp.int32)
    twos = (amount - 1) // 2
    giver, taker = sizes[1:1 + 2 * twos:2], sizes[2:2 + 2 * twos:2]
    margin = jnp.minimum(giver - 1, reach - taker)
    passed = jax.random.randint(jax.random.fold_in(own_key, 1), (twos,), 0, 1 << 20) % (margin + 1)
    sizes = sizes.at[1:1 + 2 * twos:2].set(giver - passed).at[2:2 + 2 * twos:2].set(taker + passed)
    return sizes[jax.random.permutation(jax.random.fold_in(own_key, 2), amount)]


def bell_draw(key, dims, scale, bound, cuts=(), held_as=jnp.bfloat16):
    entries = scale * jax.random.normal(key, dims, jnp.float32)
    if cuts:
        entries = entries * steps_of(key, dims, cuts, -0.22, 0.18)
    return jnp.clip(entries, -bound, bound).astype(held_as)


def setup_inputs(seed: int = 0) -> dict:
    streams_of = jax.random.split(jax.random.key(seed), 16)
    return {
        "suffix_tokens": draw_suffix_tokens(jax.random.fold_in(streams_of[15], 71), 0),
        "route_lengths": jax.vmap(lambda own: uneven(own, N_REQ, CAP, MAXLEN, 2))(jax.random.split(streams_of[1], N_REQ)).reshape((N_REQ, N_REQ)).astype(jnp.int32),
        "dest_perm": jax.vmap(lambda own: jax.random.permutation(own, N_REQ))(jax.random.split(streams_of[2], N_REQ)).reshape((N_REQ, N_REQ)).astype(jnp.int32),
        "attach_points": set_ends(jax.random.randint(streams_of[3], (REQUESTS,), 2 * WINDOW, PREFIX + 1), jax.random.fold_in(streams_of[3], 1), 2 * WINDOW, PREFIX).astype(jnp.int32),
        "prefix_cache": draw_prefix_cache(jax.random.fold_in(streams_of[15], 71), 0),
        "block_of_slot": jax.random.permutation(streams_of[5], PBLOCKS).astype(jnp.int32),
        "sink_logits": jnp.clip(6.0 * jax.random.uniform(streams_of[6], (HQ,), jnp.float32) ** steps_of(streams_of[6], (HQ,), ((0, 8),), -0.2, 0.2), 0.0, 6.0),
        "attn_gain": jnp.clip(1.0 + 0.18 * jax.random.normal(streams_of[7], (D,), jnp.float32), 0.099609375, 1.8984375).astype(jnp.bfloat16),
        "w_query": bell_draw(streams_of[8], (D, HQ * HD), D ** -0.5, 0.109375, ((1, 8),)),
        "w_keyval": bell_draw(streams_of[9], (D, KVH, 2 * HD), D ** -0.5, 0.109375, ((1, 8),)),
        "w_out": bell_draw(streams_of[10], (HQ * HD, D), (HQ * HD) ** -0.5, 0.09375, ((0, 8),)),
        "mlp_gain": jnp.clip(1.0 + 0.18 * jax.random.normal(streams_of[11], (D,), jnp.float32), 0.099609375, 1.8984375).astype(jnp.bfloat16),
        "w_gate": bell_draw(streams_of[12], (D, FF), D ** -0.5, 0.109375, ((1, 8),)),
        "w_up": bell_draw(streams_of[13], (D, FF), D ** -0.5, 0.109375, ((1, 8),)),
        "w_down": bell_draw(streams_of[14], (FF, D), FF ** -0.5, 0.109375, ((0, 8),)),
    }


ROPE_BASE = 150000.0
EPSILON = 1e-05

def norm_rows(inputs, gains):
    widened = inputs.astype(jnp.float32)
    factor = lax.rsqrt(lax.optimization_barrier(jnp.mean(widened * widened, axis=-1, keepdims=True)) + EPSILON)
    return (widened * factor * gains.astype(jnp.float32)).astype(jnp.bfloat16)

def rotate(vectors, positions):
    half_dim = vectors.shape[-1] // 2
    frequency = ROPE_BASE ** (-(jnp.arange(half_dim).astype(jnp.float32) * 2.0 / vectors.shape[-1]))
    angles = positions.astype(jnp.float32)[:, None, None] * frequency
    cosine = jnp.cos(angles)
    sine_part = jnp.sin(angles)
    first_half = vectors[..., :half_dim]
    second = vectors[..., half_dim:]
    return jnp.concatenate([first_half * cosine - second * sine_part, second * cosine + first_half * sine_part], axis=-1)

def grouped_product(left, right, groups):
    width_part = left.shape[1] // groups
    summed = jnp.zeros((left.shape[0], right.shape[1]), jnp.float32)
    for column_group in range(groups):
        lower = column_group * width_part
        piece_sum = jnp.dot(left[:, lower:lower + width_part], right[lower:lower + width_part], preferred_element_type=jnp.float32)
        summed = summed + lax.optimization_barrier(piece_sum.astype(jnp.bfloat16)).astype(jnp.float32)
    return summed

def reference(suffix_tokens, route_lengths, dest_perm, attach_points, prefix_cache, block_of_slot, sink_logits, attn_gain, w_query, w_keyval, w_out, mlp_gain, w_gate, w_up, w_down):
    peers = route_lengths.shape[0]
    requests, slot_length, features = suffix_tokens.shape
    query_heads = sink_logits.shape[0]
    value_heads = w_keyval.shape[1]
    head_dim = w_keyval.shape[2] // 2
    group_size = query_heads // value_heads
    lengths = route_lengths[dest_perm, jnp.arange(peers)[:, None]].reshape(requests).astype(jnp.int32)
    live_total = peers * CAP
    run_ends = jnp.cumsum(lengths).astype(jnp.int32)
    starts = run_ends - lengths
    packed_ids = jnp.arange(live_total).astype(jnp.int32)
    source_of = lax.optimization_barrier(jnp.sum((run_ends[None, :] <= packed_ids[:, None]).astype(jnp.int32), axis=1))
    token_index = packed_ids - starts[source_of]
    positions = attach_points[source_of] + token_index
    input_rows = suffix_tokens[source_of, token_index]
    normed_in = norm_rows(input_rows, attn_gain)
    queries = jnp.dot(normed_in, w_query, preferred_element_type=jnp.float32).reshape(live_total, query_heads, head_dim)
    queries = rotate(queries, positions).astype(jnp.bfloat16)
    paired = jnp.dot(normed_in, w_keyval.reshape(features, -1), preferred_element_type=jnp.float32).reshape(live_total, value_heads, 2 * head_dim)
    rotated = rotate(paired[..., :head_dim], positions)
    paired = jnp.concatenate([rotated, paired[..., head_dim:]], axis=-1).astype(jnp.bfloat16)
    slot_steps = jnp.arange(slot_length).astype(jnp.int32)
    slot_source = jnp.clip(starts[:, None] + slot_steps[None, :], 0, live_total - 1)
    query_slots = queries[slot_source]
    paired_slots = paired[slot_source]
    prefix = jnp.zeros_like(prefix_cache).at[block_of_slot].set(prefix_cache).reshape(-1, value_heads, 2 * head_dim)
    sink_bias = sink_logits.astype(jnp.float32).reshape(value_heads, group_size)[:, :, None, None]
    tail_steps = jnp.arange(WINDOW)
    allowed = jnp.concatenate([tail_steps[None, :] > slot_steps[:, None], slot_steps[None, :] <= slot_steps[:, None]], axis=1)

    def one_request(request_data):
        query_block, paired_block, attach = request_data
        tail_rows = lax.dynamic_slice_in_dim(prefix, (attach - WINDOW).astype(jnp.int32), WINDOW, 0)
        all_keys = jnp.concatenate([tail_rows, paired_block], axis=0).astype(jnp.float32)
        grouped_query = query_block.reshape(slot_length, value_heads, group_size, head_dim).astype(jnp.float32)
        scores = jnp.einsum('tkgd,skd->kgts', grouped_query, all_keys[..., :head_dim]) * head_dim ** (-0.5)
        scores = jnp.where(allowed, scores, -jnp.inf)
        largest = jnp.maximum(lax.optimization_barrier(jnp.max(scores, axis=-1, keepdims=True)), sink_bias)
        weights = jnp.exp(scores - largest)
        total = lax.optimization_barrier(jnp.sum(weights, axis=-1, keepdims=True)) + jnp.exp(sink_bias - largest)
        weights = (weights / total).astype(jnp.bfloat16)
        mixed = jnp.einsum('kgts,skd->tkgd', weights.astype(jnp.float32), all_keys[..., head_dim:])
        return mixed.astype(jnp.bfloat16).reshape(slot_length, query_heads * head_dim)
    attended_slots = lax.map(one_request, (query_slots, paired_slots, attach_points))
    attended = attended_slots[source_of, token_index]
    proj = grouped_product(attended, w_out, N_TP)
    residual = (input_rows.astype(jnp.float32) + proj).astype(jnp.bfloat16)
    normed_mid = norm_rows(residual, mlp_gain)
    gate_proj = jnp.dot(normed_mid, w_gate, preferred_element_type=jnp.float32)
    up_proj = jnp.dot(normed_mid, w_up, preferred_element_type=jnp.float32)
    hidden = (jax.nn.silu(gate_proj) * up_proj).astype(jnp.bfloat16)
    down_sum = grouped_product(hidden, w_down, N_TP)
    out_rows = (residual.astype(jnp.float32) + down_sum).astype(jnp.bfloat16)
    return jnp.zeros((requests, slot_length, features), jnp.bfloat16).at[source_of, token_index].set(out_rows)
```

```python
import jax
import jax.numpy as jnp
from jax import lax
from jax.sharding import PartitionSpec as P

WINDOW = 128
CAP = 768


ROPE_BASE = 150000.0
EPSILON = 1e-05


def norm_rows(inputs, gains):
    widened = inputs.astype(jnp.float32)
    factor = lax.rsqrt(jnp.mean(widened * widened, axis=-1, keepdims=True) + EPSILON)
    return (widened * factor * gains.astype(jnp.float32)).astype(jnp.bfloat16)


def rotate(vectors, positions):
    half_dim = vectors.shape[-1] // 2
    frequency = ROPE_BASE ** (-(jnp.arange(half_dim).astype(jnp.float32) * 2.0 / vectors.shape[-1]))
    angles = positions.astype(jnp.float32)[:, None, None] * frequency
    cosine = jnp.cos(angles)
    sine_part = jnp.sin(angles)
    first_half = vectors[..., :half_dim]
    second = vectors[..., half_dim:]
    return jnp.concatenate(
        [first_half * cosine - second * sine_part, second * cosine + first_half * sine_part],
        axis=-1,
    )


def attend(query_slots, paired_slots, tail_rows, sink_logits):
    peers, slot_length = (query_slots.shape[0], query_slots.shape[1])
    value_heads = paired_slots.shape[2]
    head_dim = paired_slots.shape[3] // 2
    group_size = query_slots.shape[2] // value_heads
    window = tail_rows.shape[1]
    grouped_query = query_slots.reshape(peers, slot_length, value_heads, group_size, head_dim)
    near_keys = jnp.concatenate([tail_rows, paired_slots], axis=1)
    score_scale = head_dim ** (-0.5)
    near_scores = (
        jnp.einsum(
            "ntkgd,nskd->nkgts",
            grouped_query,
            near_keys[..., :head_dim],
            preferred_element_type=jnp.float32,
        )
        * score_scale
    )
    sink_scores = sink_logits.reshape(value_heads, group_size)[None, :, :, None, None]
    slot_steps = jnp.arange(slot_length)
    columns = jnp.arange(window + slot_length)
    allowed = jnp.where(
        columns[None, :] < window,
        columns[None, :] > slot_steps[:, None],
        columns[None, :] - window <= slot_steps[:, None],
    )
    near_scores = jnp.where(allowed, near_scores, -jnp.inf)
    largest = jnp.maximum(jnp.max(near_scores, axis=-1, keepdims=True), sink_scores)
    near_weights = jnp.exp(near_scores - largest)
    normalizer = jnp.sum(near_weights, axis=-1, keepdims=True) + jnp.exp(sink_scores - largest)
    near_weights = (near_weights / normalizer).astype(jnp.bfloat16)
    mixed = jnp.einsum(
        "nkgts,nskd->ntkgd",
        near_weights,
        near_keys[..., head_dim:],
        preferred_element_type=jnp.float32,
    )
    return mixed.astype(jnp.bfloat16).reshape(
        peers * slot_length, value_heads * group_size * head_dim
    )


def fetch_prefix(attach_slots, prefix_cache, block_of_slot, window):
    total_blocks = block_of_slot.shape[0]
    block_len = prefix_cache.shape[1]
    catalog = jnp.arange(total_blocks)
    home_row = jnp.sum(
        jnp.where(block_of_slot[None, :] == catalog[:, None], catalog[None, :], 0), axis=1
    )
    wanted = attach_slots[:, None] - window + jnp.arange(window)[None, :]
    block_id = wanted // block_len
    tail_store = jnp.sum(jnp.where(block_id[..., None] == catalog, home_row, 0), axis=-1)
    tail_offset = wanted - block_id * block_len
    trailing = prefix_cache.shape[2:]
    initial = jnp.zeros((attach_slots.shape[0], window) + trailing, jnp.bfloat16)
    shard_rows = lax.all_gather(prefix_cache, "req", axis=0, tiled=True)
    held_blocks = shard_rows.shape[0]
    flat_rows = shard_rows.reshape((held_blocks * block_len,) + trailing)
    inside = (tail_store >= 0) & (tail_store < held_blocks)
    picked = flat_rows[jnp.clip(tail_store, 0, held_blocks - 1) * block_len + tail_offset]
    return jnp.where(inside[..., None, None], picked, initial)


def norm_groups(parts, gains):
    widened = parts.astype(jnp.float32)
    total = jnp.sum(widened * widened, axis=(0, 2), keepdims=True)
    factor = lax.rsqrt(total / (parts.shape[0] * parts.shape[2]) + EPSILON)
    return (widened * factor * gains.astype(jnp.float32)).astype(jnp.bfloat16)


def group_dot(parts, weight):
    groups, _, share = parts.shape
    return jnp.einsum(
        "gtf,gfo->to",
        parts,
        weight.reshape((groups, share) + weight.shape[1:]),
        preferred_element_type=jnp.float32,
    )


def local(
    suffix_tokens,
    route_lengths,
    dest_perm,
    attach_points,
    prefix_cache,
    block_of_slot,
    sink_logits,
    attn_gain,
    w_query,
    w_keyval,
    w_out,
    mlp_gain,
    w_gate,
    w_up,
    w_down,
):
    peers = lax.axis_size("req")
    splits = lax.axis_size("tp")
    request_index = lax.axis_index("req")
    tensor_index = lax.axis_index("tp")
    slot_count, slot_length, features = suffix_tokens.shape
    feature_share = features // splits
    value_heads = w_keyval.shape[1]
    head_dim = w_keyval.shape[2] // 2
    peer_ids = jnp.arange(peers)
    slot_steps = jnp.arange(slot_length)
    my_row = lax.dynamic_index_in_dim(dest_perm, request_index, 0, keepdims=False)
    attach_table = attach_points.reshape(peers, peers)
    arriving_lengths = lax.dynamic_index_in_dim(route_lengths, request_index, 0, keepdims=False)
    arriving = (dest_perm == request_index).astype(jnp.int32)
    arriving_attach = jnp.sum(attach_table * arriving, axis=1)
    send_order = jnp.sum(
        jnp.where(my_row[None, :] == peer_ids[:, None], peer_ids[None, :], 0), axis=1
    )
    run_ends = jnp.cumsum(arriving_lengths)
    starts = run_ends - arriving_lengths
    packed_ids = jnp.arange(CAP)
    source_of = jnp.sum((run_ends[None, :] <= packed_ids[:, None]).astype(jnp.int32), axis=1)
    source_hot = (source_of[:, None] == peer_ids[None, :]).astype(jnp.int32)
    token_index = packed_ids - jnp.sum(source_hot * starts[None, :], axis=1)
    positions = jnp.sum(source_hot * arriving_attach[None, :], axis=1) + token_index
    flat_index = source_of * slot_length + token_index
    slot_source = jnp.clip(starts[:, None] + slot_steps[None, :], 0, CAP - 1).reshape(-1)
    live_mask = slot_steps[None, :] < arriving_lengths[:, None]

    def to_slots(values):
        return values[slot_source].reshape((peers, slot_length) + values.shape[1:])

    tail_rows = fetch_prefix(arriving_attach, prefix_cache, block_of_slot, WINDOW)
    my_features = lax.dynamic_slice_in_dim(
        suffix_tokens, tensor_index * feature_share, feature_share, 2
    )
    landed = lax.all_to_all(
        my_features[send_order], "req", split_axis=0, concat_axis=0, tiled=True
    )
    input_part = landed.reshape(peers * slot_length, feature_share)[flat_index]
    input_groups = lax.all_gather(input_part, "tp", axis=0, tiled=False)
    row_total = input_part.shape[0]
    normed_in = norm_groups(input_groups, attn_gain.reshape(splits, 1, feature_share))
    queries = group_dot(normed_in, w_query).reshape(row_total, -1, head_dim)
    queries = rotate(queries, positions).astype(jnp.bfloat16)
    paired = group_dot(normed_in, w_keyval.reshape(features, -1)).reshape(
        row_total, value_heads, 2 * head_dim
    )
    rotated = rotate(paired[..., :head_dim], positions)
    paired = jnp.concatenate([rotated, paired[..., head_dim:]], axis=-1).astype(jnp.bfloat16)
    attended = attend(to_slots(queries), to_slots(paired), tail_rows, sink_logits)[flat_index]
    partial_value = jnp.dot(attended, w_out, preferred_element_type=jnp.float32)
    summed = lax.psum_scatter(
        partial_value.astype(jnp.bfloat16), "tp", scatter_dimension=1, tiled=True
    ).astype(jnp.float32)
    residual_part = (input_part.astype(jnp.float32) + summed).astype(jnp.bfloat16)
    residual_groups = lax.all_gather(residual_part, "tp", axis=0, tiled=False)
    normed_mid = norm_groups(residual_groups, mlp_gain.reshape(splits, 1, feature_share))
    gate_proj = group_dot(normed_mid, w_gate)
    up_proj = group_dot(normed_mid, w_up)
    hidden = (jax.nn.silu(gate_proj) * up_proj).astype(jnp.bfloat16)
    down_sum = lax.psum_scatter(
        jnp.dot(hidden, w_down, preferred_element_type=jnp.float32).astype(jnp.bfloat16),
        "tp",
        scatter_dimension=1,
        tiled=True,
    ).astype(jnp.float32)
    out_rows = (residual_part.astype(jnp.float32) + down_sum).astype(jnp.bfloat16)
    out_slots = jnp.where(live_mask[..., None], to_slots(out_rows), jnp.zeros((), jnp.bfloat16))
    returned = lax.all_to_all(out_slots, "req", split_axis=0, concat_axis=0, tiled=True)
    return returned[my_row]


def solution(mesh):
    in_specs = (
        P("req", None, None),
        P(),
        P(),
        P(),
        P("req", None, "tp", None),
        P(),
        P("tp"),
        P(),
        P(None, "tp"),
        P(None, "tp", None),
        P("tp", None),
        P(),
        P(None, "tp"),
        P(None, "tp"),
        P("tp", None),
    )
    out_specs = P("req", None, "tp")
    return jax.shard_map(local, mesh=mesh, in_specs=in_specs, out_specs=out_specs, check_vma=False)
```

```python
import jax
import jax.numpy as jnp
from jax import lax
from jax.sharding import PartitionSpec as P
from jax.experimental import pallas as pl
from jax.experimental.pallas import tpu as pltpu

WINDOW = 128
CAP = 768


ROPE_BASE = 150000.0
EPSILON = 1e-05


def norm_rows(inputs, gains):
    widened = inputs.astype(jnp.float32)
    factor = lax.rsqrt(jnp.mean(widened * widened, axis=-1, keepdims=True) + EPSILON)
    return (widened * factor * gains.astype(jnp.float32)).astype(jnp.bfloat16)


def rotate(vectors, positions):
    half_dim = vectors.shape[-1] // 2
    frequency = ROPE_BASE ** (-(jnp.arange(half_dim).astype(jnp.float32) * 2.0 / vectors.shape[-1]))
    angles = positions.astype(jnp.float32)[:, None, None] * frequency
    cosine = jnp.cos(angles)
    sine_part = jnp.sin(angles)
    first_half = vectors[..., :half_dim]
    second = vectors[..., half_dim:]
    return jnp.concatenate(
        [first_half * cosine - second * sine_part, second * cosine + first_half * sine_part],
        axis=-1,
    )


def attend(query_slots, paired_slots, tail_rows, sink_logits):
    peers, slot_length = (query_slots.shape[0], query_slots.shape[1])
    value_heads = paired_slots.shape[2]
    head_dim = paired_slots.shape[3] // 2
    group_size = query_slots.shape[2] // value_heads
    window = tail_rows.shape[1]
    grouped_query = query_slots.reshape(peers, slot_length, value_heads, group_size, head_dim)
    near_keys = jnp.concatenate([tail_rows, paired_slots], axis=1)
    score_scale = head_dim ** (-0.5)
    near_scores = (
        jnp.einsum(
            "ntkgd,nskd->nkgts",
            grouped_query,
            near_keys[..., :head_dim],
            preferred_element_type=jnp.float32,
        )
        * score_scale
    )
    sink_scores = sink_logits.reshape(value_heads, group_size)[None, :, :, None, None]
    slot_steps = jnp.arange(slot_length)
    columns = jnp.arange(window + slot_length)
    allowed = jnp.where(
        columns[None, :] < window,
        columns[None, :] > slot_steps[:, None],
        columns[None, :] - window <= slot_steps[:, None],
    )
    near_scores = jnp.where(allowed, near_scores, -jnp.inf)
    largest = jnp.maximum(jnp.max(near_scores, axis=-1, keepdims=True), sink_scores)
    near_weights = jnp.exp(near_scores - largest)
    normalizer = jnp.sum(near_weights, axis=-1, keepdims=True) + jnp.exp(sink_scores - largest)
    near_weights = (near_weights / normalizer).astype(jnp.bfloat16)
    mixed = jnp.einsum(
        "nkgts,nskd->ntkgd",
        near_weights,
        near_keys[..., head_dim:],
        preferred_element_type=jnp.float32,
    )
    return mixed.astype(jnp.bfloat16).reshape(
        peers * slot_length, value_heads * group_size * head_dim
    )


def attend_kernel(sink_ref, q_ref, kv_ref, tail_ref, o_ref):
    slot_length = q_ref.shape[1]
    window = tail_ref.shape[1]
    head_dim = kv_ref.shape[2] // 2
    heads = q_ref.shape[2] // head_dim
    scale = head_dim ** (-0.5)
    kv = kv_ref[0]
    tail = tail_ref[0]
    own_keys, own_values = kv[:, :head_dim], kv[:, head_dim:]
    tail_keys, tail_values = tail[:, :head_dim], tail[:, head_dim:]
    step = lax.broadcasted_iota(jnp.int32, (slot_length, window), 0)
    column = lax.broadcasted_iota(jnp.int32, (slot_length, window), 1)
    tail_allowed = column > step
    own_step = lax.broadcasted_iota(jnp.int32, (slot_length, slot_length), 0)
    own_column = lax.broadcasted_iota(jnp.int32, (slot_length, slot_length), 1)
    own_allowed = own_column <= own_step
    contract = (((1,), (1,)), ((), ()))
    for head in range(heads):
        query = q_ref[0, :, head * head_dim:(head + 1) * head_dim]
        tail_scores = lax.dot_general(
            query, tail_keys, contract, preferred_element_type=jnp.float32
        ) * scale
        own_scores = lax.dot_general(
            query, own_keys, contract, preferred_element_type=jnp.float32
        ) * scale
        tail_scores = jnp.where(tail_allowed, tail_scores, -jnp.inf)
        own_scores = jnp.where(own_allowed, own_scores, -jnp.inf)
        sink = sink_ref[head]
        largest = jnp.maximum(
            jnp.maximum(
                jnp.max(tail_scores, axis=1, keepdims=True),
                jnp.max(own_scores, axis=1, keepdims=True),
            ),
            sink,
        )
        tail_weights = jnp.exp(tail_scores - largest)
        own_weights = jnp.exp(own_scores - largest)
        normalizer = (
            jnp.sum(tail_weights, axis=1, keepdims=True)
            + jnp.sum(own_weights, axis=1, keepdims=True)
            + jnp.exp(sink - largest)
        )
        tail_weights = (tail_weights / normalizer).astype(jnp.bfloat16)
        own_weights = (own_weights / normalizer).astype(jnp.bfloat16)
        mixed = jnp.dot(
            tail_weights, tail_values, preferred_element_type=jnp.float32
        ) + jnp.dot(own_weights, own_values, preferred_element_type=jnp.float32)
        o_ref[0, :, head * head_dim:(head + 1) * head_dim] = mixed.astype(o_ref.dtype)


def attend_pallas(query_slots, paired_slots, tail_rows, sink_logits):
    peers, slot_length, width = query_slots.shape
    window = tail_rows.shape[1]
    pair_width = paired_slots.shape[2]
    head_dim = pair_width // 2
    heads = width // head_dim
    flops = peers * heads * 4 * slot_length * (window + slot_length) * head_dim
    moved = 2 * (2 * query_slots.size + paired_slots.size + tail_rows.size)
    return pl.pallas_call(
        attend_kernel,
        grid=(peers,),
        in_specs=[
            pl.BlockSpec(memory_space=pltpu.SMEM),
            pl.BlockSpec((1, slot_length, width), lambda n: (n, 0, 0)),
            pl.BlockSpec((1, slot_length, pair_width), lambda n: (n, 0, 0)),
            pl.BlockSpec((1, window, pair_width), lambda n: (n, 0, 0)),
        ],
        out_specs=pl.BlockSpec((1, slot_length, width), lambda n: (n, 0, 0)),
        out_shape=jax.ShapeDtypeStruct((peers, slot_length, width), jnp.bfloat16),
        cost_estimate=pl.CostEstimate(
            flops=flops,
            transcendentals=peers * heads * slot_length * (window + slot_length),
            bytes_accessed=moved,
        ),
    )(sink_logits.astype(jnp.float32), query_slots, paired_slots, tail_rows)


def fetch_prefix(attach_slots, prefix_cache, block_of_slot, window):
    total_blocks = block_of_slot.shape[0]
    block_len = prefix_cache.shape[1]
    catalog = jnp.arange(total_blocks)
    home_row = jnp.sum(
        jnp.where(block_of_slot[None, :] == catalog[:, None], catalog[None, :], 0), axis=1
    )
    wanted = attach_slots[:, None] - window + jnp.arange(window)[None, :]
    block_id = wanted // block_len
    tail_store = jnp.sum(jnp.where(block_id[..., None] == catalog, home_row, 0), axis=-1)
    tail_offset = wanted - block_id * block_len
    trailing = prefix_cache.shape[2:]
    initial = jnp.zeros((attach_slots.shape[0], window) + trailing, jnp.bfloat16)
    shard_rows = lax.all_gather(prefix_cache, "req", axis=0, tiled=True)
    held_blocks = shard_rows.shape[0]
    flat_rows = shard_rows.reshape((held_blocks * block_len,) + trailing)
    inside = (tail_store >= 0) & (tail_store < held_blocks)
    picked = flat_rows[jnp.clip(tail_store, 0, held_blocks - 1) * block_len + tail_offset]
    return jnp.where(inside[..., None, None], picked, initial)


def norm_groups(parts, gains):
    widened = parts.astype(jnp.float32)
    total = jnp.sum(widened * widened, axis=(0, 2), keepdims=True)
    factor = lax.rsqrt(total / (parts.shape[0] * parts.shape[2]) + EPSILON)
    return (widened * factor * gains.astype(jnp.float32)).astype(jnp.bfloat16)


def group_dot(parts, weight):
    groups, _, share = parts.shape
    return jnp.einsum(
        "gtf,gfo->to",
        parts,
        weight.reshape((groups, share) + weight.shape[1:]),
        preferred_element_type=jnp.float32,
    )


def local(
    suffix_tokens,
    route_lengths,
    dest_perm,
    attach_points,
    prefix_cache,
    block_of_slot,
    sink_logits,
    attn_gain,
    w_query,
    w_keyval,
    w_out,
    mlp_gain,
    w_gate,
    w_up,
    w_down,
):
    peers = lax.axis_size("req")
    splits = lax.axis_size("tp")
    request_index = lax.axis_index("req")
    tensor_index = lax.axis_index("tp")
    slot_count, slot_length, features = suffix_tokens.shape
    feature_share = features // splits
    value_heads = w_keyval.shape[1]
    head_dim = w_keyval.shape[2] // 2
    peer_ids = jnp.arange(peers)
    slot_steps = jnp.arange(slot_length)
    my_row = lax.dynamic_index_in_dim(dest_perm, request_index, 0, keepdims=False)
    attach_table = attach_points.reshape(peers, peers)
    arriving_lengths = lax.dynamic_index_in_dim(route_lengths, request_index, 0, keepdims=False)
    arriving = (dest_perm == request_index).astype(jnp.int32)
    arriving_attach = jnp.sum(attach_table * arriving, axis=1)
    send_order = jnp.sum(
        jnp.where(my_row[None, :] == peer_ids[:, None], peer_ids[None, :], 0), axis=1
    )
    run_ends = jnp.cumsum(arriving_lengths)
    starts = run_ends - arriving_lengths
    packed_ids = jnp.arange(CAP)
    source_of = jnp.sum((run_ends[None, :] <= packed_ids[:, None]).astype(jnp.int32), axis=1)
    source_hot = (source_of[:, None] == peer_ids[None, :]).astype(jnp.int32)
    token_index = packed_ids - jnp.sum(source_hot * starts[None, :], axis=1)
    positions = jnp.sum(source_hot * arriving_attach[None, :], axis=1) + token_index
    flat_index = source_of * slot_length + token_index
    slot_source = jnp.clip(starts[:, None] + slot_steps[None, :], 0, CAP - 1).reshape(-1)
    live_mask = slot_steps[None, :] < arriving_lengths[:, None]

    def to_slots(values):
        return values[slot_source].reshape((peers, slot_length) + values.shape[1:])

    tail_rows = fetch_prefix(arriving_attach, prefix_cache, block_of_slot, WINDOW)
    my_features = lax.dynamic_slice_in_dim(
        suffix_tokens, tensor_index * feature_share, feature_share, 2
    )
    landed = lax.all_to_all(
        my_features[send_order], "req", split_axis=0, concat_axis=0, tiled=True
    )
    input_part = landed.reshape(peers * slot_length, feature_share)[flat_index]
    input_groups = lax.all_gather(input_part, "tp", axis=0, tiled=False)
    row_total = input_part.shape[0]
    normed_in = norm_groups(input_groups, attn_gain.reshape(splits, 1, feature_share))
    queries = group_dot(normed_in, w_query).reshape(row_total, -1, head_dim)
    queries = rotate(queries, positions).astype(jnp.bfloat16)
    paired = group_dot(normed_in, w_keyval.reshape(features, -1)).reshape(
        row_total, value_heads, 2 * head_dim
    )
    rotated = rotate(paired[..., :head_dim], positions)
    paired = jnp.concatenate([rotated, paired[..., head_dim:]], axis=-1).astype(jnp.bfloat16)
    attended = attend_pallas(
        to_slots(queries.reshape(row_total, -1)),
        to_slots(paired.reshape(row_total, -1)),
        tail_rows.reshape(peers, WINDOW, -1),
        sink_logits,
    ).reshape(peers * slot_length, -1)[flat_index]
    partial_value = jnp.dot(attended, w_out, preferred_element_type=jnp.float32)
    summed = lax.psum_scatter(
        partial_value.astype(jnp.bfloat16), "tp", scatter_dimension=1, tiled=True
    ).astype(jnp.float32)
    residual_part = (input_part.astype(jnp.float32) + summed).astype(jnp.bfloat16)
    residual_groups = lax.all_gather(residual_part, "tp", axis=0, tiled=False)
    normed_mid = norm_groups(residual_groups, mlp_gain.reshape(splits, 1, feature_share))
    gate_proj = group_dot(normed_mid, w_gate)
    up_proj = group_dot(normed_mid, w_up)
    hidden = (jax.nn.silu(gate_proj) * up_proj).astype(jnp.bfloat16)
    down_sum = lax.psum_scatter(
        jnp.dot(hidden, w_down, preferred_element_type=jnp.float32).astype(jnp.bfloat16),
        "tp",
        scatter_dimension=1,
        tiled=True,
    ).astype(jnp.float32)
    out_rows = (residual_part.astype(jnp.float32) + down_sum).astype(jnp.bfloat16)
    out_slots = jnp.where(live_mask[..., None], to_slots(out_rows), jnp.zeros((), jnp.bfloat16))
    returned = lax.all_to_all(out_slots, "req", split_axis=0, concat_axis=0, tiled=True)
    return returned[my_row]


def solution(mesh):
    in_specs = (
        P("req", None, None),
        P(),
        P(),
        P(),
        P("req", None, "tp", None),
        P(),
        P("tp"),
        P(),
        P(None, "tp"),
        P(None, "tp", None),
        P("tp", None),
        P(),
        P(None, "tp"),
        P(None, "tp"),
        P("tp", None),
    )
    out_specs = P("req", None, "tp")
    return jax.shard_map(local, mesh=mesh, in_specs=in_specs, out_specs=out_specs, check_vma=False)
```

```python
import jax
import jax.numpy as jnp
from jax import lax
from jax.sharding import PartitionSpec as P
from jax.experimental import pallas as pl
from jax.experimental.pallas import tpu as pltpu

WINDOW = 128
CAP = 768


ROPE_BASE = 150000.0
EPSILON = 1e-05


def norm_rows(inputs, gains):
    widened = inputs.astype(jnp.float32)
    factor = lax.rsqrt(jnp.mean(widened * widened, axis=-1, keepdims=True) + EPSILON)
    return (widened * factor * gains.astype(jnp.float32)).astype(jnp.bfloat16)


def rotate(vectors, positions):
    half_dim = vectors.shape[-1] // 2
    frequency = ROPE_BASE ** (-(jnp.arange(half_dim).astype(jnp.float32) * 2.0 / vectors.shape[-1]))
    angles = positions.astype(jnp.float32)[:, None, None] * frequency
    cosine = jnp.cos(angles)
    sine_part = jnp.sin(angles)
    first_half = vectors[..., :half_dim]
    second = vectors[..., half_dim:]
    return jnp.concatenate(
        [first_half * cosine - second * sine_part, second * cosine + first_half * sine_part],
        axis=-1,
    )


def attend(query_slots, paired_slots, tail_rows, sink_logits):
    peers, slot_length = (query_slots.shape[0], query_slots.shape[1])
    value_heads = paired_slots.shape[2]
    head_dim = paired_slots.shape[3] // 2
    group_size = query_slots.shape[2] // value_heads
    window = tail_rows.shape[1]
    grouped_query = query_slots.reshape(peers, slot_length, value_heads, group_size, head_dim)
    near_keys = jnp.concatenate([tail_rows, paired_slots], axis=1)
    score_scale = head_dim ** (-0.5)
    near_scores = (
        jnp.einsum(
            "ntkgd,nskd->nkgts",
            grouped_query,
            near_keys[..., :head_dim],
            preferred_element_type=jnp.float32,
        )
        * score_scale
    )
    sink_scores = sink_logits.reshape(value_heads, group_size)[None, :, :, None, None]
    slot_steps = jnp.arange(slot_length)
    columns = jnp.arange(window + slot_length)
    allowed = jnp.where(
        columns[None, :] < window,
        columns[None, :] > slot_steps[:, None],
        columns[None, :] - window <= slot_steps[:, None],
    )
    near_scores = jnp.where(allowed, near_scores, -jnp.inf)
    largest = jnp.maximum(jnp.max(near_scores, axis=-1, keepdims=True), sink_scores)
    near_weights = jnp.exp(near_scores - largest)
    normalizer = jnp.sum(near_weights, axis=-1, keepdims=True) + jnp.exp(sink_scores - largest)
    near_weights = (near_weights / normalizer).astype(jnp.bfloat16)
    mixed = jnp.einsum(
        "nkgts,nskd->ntkgd",
        near_weights,
        near_keys[..., head_dim:],
        preferred_element_type=jnp.float32,
    )
    return mixed.astype(jnp.bfloat16).reshape(
        peers * slot_length, value_heads * group_size * head_dim
    )


def attend_kernel(sink_ref, q_ref, kv_ref, tail_ref, o_ref):
    slot_length = q_ref.shape[1]
    window = tail_ref.shape[1]
    head_dim = kv_ref.shape[2] // 2
    heads = q_ref.shape[2] // head_dim
    scale = head_dim ** (-0.5)
    kv = kv_ref[0]
    tail = tail_ref[0]
    own_keys, own_values = kv[:, :head_dim], kv[:, head_dim:]
    tail_keys, tail_values = tail[:, :head_dim], tail[:, head_dim:]
    step = lax.broadcasted_iota(jnp.int32, (slot_length, window), 0)
    column = lax.broadcasted_iota(jnp.int32, (slot_length, window), 1)
    tail_allowed = column > step
    own_step = lax.broadcasted_iota(jnp.int32, (slot_length, slot_length), 0)
    own_column = lax.broadcasted_iota(jnp.int32, (slot_length, slot_length), 1)
    own_allowed = own_column <= own_step
    contract = (((1,), (1,)), ((), ()))
    for head in range(heads):
        query = q_ref[0, :, head * head_dim:(head + 1) * head_dim]
        tail_scores = lax.dot_general(
            query, tail_keys, contract, preferred_element_type=jnp.float32
        ) * scale
        own_scores = lax.dot_general(
            query, own_keys, contract, preferred_element_type=jnp.float32
        ) * scale
        tail_scores = jnp.where(tail_allowed, tail_scores, -jnp.inf)
        own_scores = jnp.where(own_allowed, own_scores, -jnp.inf)
        sink = sink_ref[head]
        largest = jnp.maximum(
            jnp.maximum(
                jnp.max(tail_scores, axis=1, keepdims=True),
                jnp.max(own_scores, axis=1, keepdims=True),
            ),
            sink,
        )
        tail_weights = jnp.exp(tail_scores - largest)
        own_weights = jnp.exp(own_scores - largest)
        normalizer = (
            jnp.sum(tail_weights, axis=1, keepdims=True)
            + jnp.sum(own_weights, axis=1, keepdims=True)
            + jnp.exp(sink - largest)
        )
        tail_weights = (tail_weights / normalizer).astype(jnp.bfloat16)
        own_weights = (own_weights / normalizer).astype(jnp.bfloat16)
        mixed = jnp.dot(
            tail_weights, tail_values, preferred_element_type=jnp.float32
        ) + jnp.dot(own_weights, own_values, preferred_element_type=jnp.float32)
        o_ref[0, :, head * head_dim:(head + 1) * head_dim] = mixed.astype(o_ref.dtype)


def attend_pallas(query_slots, paired_slots, tail_rows, sink_logits):
    peers, slot_length, width = query_slots.shape
    window = tail_rows.shape[1]
    pair_width = paired_slots.shape[2]
    head_dim = pair_width // 2
    heads = width // head_dim
    flops = peers * heads * 4 * slot_length * (window + slot_length) * head_dim
    moved = 2 * (2 * query_slots.size + paired_slots.size + tail_rows.size)
    return pl.pallas_call(
        attend_kernel,
        grid=(peers,),
        in_specs=[
            pl.BlockSpec(memory_space=pltpu.SMEM),
            pl.BlockSpec((1, slot_length, width), lambda n: (n, 0, 0)),
            pl.BlockSpec((1, slot_length, pair_width), lambda n: (n, 0, 0)),
            pl.BlockSpec((1, window, pair_width), lambda n: (n, 0, 0)),
        ],
        out_specs=pl.BlockSpec((1, slot_length, width), lambda n: (n, 0, 0)),
        out_shape=jax.ShapeDtypeStruct((peers, slot_length, width), jnp.bfloat16),
        cost_estimate=pl.CostEstimate(
            flops=flops,
            transcendentals=peers * heads * slot_length * (window + slot_length),
            bytes_accessed=moved,
        ),
    )(sink_logits.astype(jnp.float32), query_slots, paired_slots, tail_rows)


def fetch_prefix(attach_slots, prefix_cache, block_of_slot, window):
    total_blocks = block_of_slot.shape[0]
    block_len = prefix_cache.shape[1]
    catalog = jnp.arange(total_blocks)
    home_row = jnp.sum(
        jnp.where(block_of_slot[None, :] == catalog[:, None], catalog[None, :], 0), axis=1
    )
    wanted = attach_slots[:, None] - window + jnp.arange(window)[None, :]
    block_id = wanted // block_len
    tail_store = jnp.sum(jnp.where(block_id[..., None] == catalog, home_row, 0), axis=-1)
    tail_offset = wanted - block_id * block_len
    trailing = prefix_cache.shape[2:]
    initial = jnp.zeros((attach_slots.shape[0], window) + trailing, jnp.bfloat16)
    shard_rows = lax.all_gather(prefix_cache, "req", axis=0, tiled=True)
    held_blocks = shard_rows.shape[0]
    flat_rows = shard_rows.reshape((held_blocks * block_len,) + trailing)
    inside = (tail_store >= 0) & (tail_store < held_blocks)
    picked = flat_rows[jnp.clip(tail_store, 0, held_blocks - 1) * block_len + tail_offset]
    return jnp.where(inside[..., None, None], picked, initial)


def local(
    suffix_tokens,
    route_lengths,
    dest_perm,
    attach_points,
    prefix_cache,
    block_of_slot,
    sink_logits,
    attn_gain,
    w_query,
    w_keyval,
    w_out,
    mlp_gain,
    w_gate,
    w_up,
    w_down,
):
    peers = lax.axis_size("req")
    splits = lax.axis_size("tp")
    request_index = lax.axis_index("req")
    tensor_index = lax.axis_index("tp")
    slot_count, slot_length, features = suffix_tokens.shape
    feature_share = features // splits
    value_heads = w_keyval.shape[1]
    head_dim = w_keyval.shape[2] // 2
    peer_ids = jnp.arange(peers)
    slot_steps = jnp.arange(slot_length)
    my_row = lax.dynamic_index_in_dim(dest_perm, request_index, 0, keepdims=False)
    attach_table = attach_points.reshape(peers, peers)
    arriving_lengths = lax.dynamic_index_in_dim(route_lengths, request_index, 0, keepdims=False)
    arriving = (dest_perm == request_index).astype(jnp.int32)
    arriving_attach = jnp.sum(attach_table * arriving, axis=1)
    send_order = jnp.sum(
        jnp.where(my_row[None, :] == peer_ids[:, None], peer_ids[None, :], 0), axis=1
    )
    run_ends = jnp.cumsum(arriving_lengths)
    starts = run_ends - arriving_lengths
    packed_ids = jnp.arange(CAP)
    source_of = jnp.sum((run_ends[None, :] <= packed_ids[:, None]).astype(jnp.int32), axis=1)
    source_hot = (source_of[:, None] == peer_ids[None, :]).astype(jnp.int32)
    token_index = packed_ids - jnp.sum(source_hot * starts[None, :], axis=1)
    positions = jnp.sum(source_hot * arriving_attach[None, :], axis=1) + token_index
    flat_index = source_of * slot_length + token_index
    slot_source = jnp.clip(starts[:, None] + slot_steps[None, :], 0, CAP - 1).reshape(-1)
    live_mask = slot_steps[None, :] < arriving_lengths[:, None]

    def to_slots(values):
        return values[slot_source].reshape((peers, slot_length) + values.shape[1:])

    tail_rows = fetch_prefix(arriving_attach, prefix_cache, block_of_slot, WINDOW)
    my_features = lax.dynamic_slice_in_dim(
        suffix_tokens, tensor_index * feature_share, feature_share, 2
    )
    landed = lax.all_to_all(
        my_features[send_order], "req", split_axis=0, concat_axis=0, tiled=True
    )
    input_part = landed.reshape(peers * slot_length, feature_share)[flat_index]
    input_rows = lax.all_gather(input_part, "tp", axis=1, tiled=True)
    row_total = input_part.shape[0]
    normed_in = norm_rows(input_rows, attn_gain)
    queries = jnp.dot(normed_in, w_query, preferred_element_type=jnp.float32).reshape(
        row_total, -1, head_dim
    )
    queries = rotate(queries, positions).astype(jnp.bfloat16)
    paired = jnp.dot(
        normed_in, w_keyval.reshape(features, -1), preferred_element_type=jnp.float32
    ).reshape(row_total, value_heads, 2 * head_dim)
    rotated = rotate(paired[..., :head_dim], positions)
    paired = jnp.concatenate([rotated, paired[..., head_dim:]], axis=-1).astype(jnp.bfloat16)
    attended = attend_pallas(
        to_slots(queries.reshape(row_total, -1)),
        to_slots(paired.reshape(row_total, -1)),
        tail_rows.reshape(peers, WINDOW, -1),
        sink_logits,
    ).reshape(peers * slot_length, -1)[flat_index]
    partial_value = jnp.dot(attended, w_out, preferred_element_type=jnp.float32)
    summed = lax.psum_scatter(
        partial_value.astype(jnp.bfloat16), "tp", scatter_dimension=1, tiled=True
    ).astype(jnp.float32)
    residual_part = (input_part.astype(jnp.float32) + summed).astype(jnp.bfloat16)
    residual = lax.all_gather(residual_part, "tp", axis=1, tiled=True)
    normed_mid = norm_rows(residual, mlp_gain)
    gate_proj = jnp.dot(normed_mid, w_gate, preferred_element_type=jnp.float32)
    up_proj = jnp.dot(normed_mid, w_up, preferred_element_type=jnp.float32)
    hidden = (jax.nn.silu(gate_proj) * up_proj).astype(jnp.bfloat16)
    down_sum = lax.psum_scatter(
        jnp.dot(hidden, w_down, preferred_element_type=jnp.float32).astype(jnp.bfloat16),
        "tp",
        scatter_dimension=1,
        tiled=True,
    ).astype(jnp.float32)
    out_rows = (residual_part.astype(jnp.float32) + down_sum).astype(jnp.bfloat16)
    out_slots = jnp.where(live_mask[..., None], to_slots(out_rows), jnp.zeros((), jnp.bfloat16))
    returned = lax.all_to_all(out_slots, "req", split_axis=0, concat_axis=0, tiled=True)
    return returned[my_row]


def solution(mesh):
    in_specs = (
        P("req", None, None),
        P(),
        P(),
        P(),
        P("req", None, "tp", None),
        P(),
        P("tp"),
        P(),
        P(None, "tp"),
        P(None, "tp", None),
        P("tp", None),
        P(),
        P(None, "tp"),
        P(None, "tp"),
        P("tp", None),
    )
    out_specs = P("req", None, "tp")
    return jax.shard_map(local, mesh=mesh, in_specs=in_specs, out_specs=out_specs, check_vma=False)
```

```python
import jax
import jax.numpy as jnp
from jax import lax
from jax.sharding import PartitionSpec as P
from jax.experimental import pallas as pl
from jax.experimental.pallas import tpu as pltpu

WINDOW = 128
CAP = 768


ROPE_BASE = 150000.0
EPSILON = 1e-05


def norm_rows(inputs, gains):
    widened = inputs.astype(jnp.float32)
    factor = lax.rsqrt(jnp.mean(widened * widened, axis=-1, keepdims=True) + EPSILON)
    return (widened * factor * gains.astype(jnp.float32)).astype(jnp.bfloat16)


def rotate(vectors, positions):
    half_dim = vectors.shape[-1] // 2
    frequency = ROPE_BASE ** (-(jnp.arange(half_dim).astype(jnp.float32) * 2.0 / vectors.shape[-1]))
    angles = positions.astype(jnp.float32)[:, None, None] * frequency
    cosine = jnp.cos(angles)
    sine_part = jnp.sin(angles)
    first_half = vectors[..., :half_dim]
    second = vectors[..., half_dim:]
    return jnp.concatenate(
        [first_half * cosine - second * sine_part, second * cosine + first_half * sine_part],
        axis=-1,
    )


def attend(query_slots, paired_slots, tail_rows, sink_logits):
    peers, slot_length = (query_slots.shape[0], query_slots.shape[1])
    value_heads = paired_slots.shape[2]
    head_dim = paired_slots.shape[3] // 2
    group_size = query_slots.shape[2] // value_heads
    window = tail_rows.shape[1]
    grouped_query = query_slots.reshape(peers, slot_length, value_heads, group_size, head_dim)
    near_keys = jnp.concatenate([tail_rows, paired_slots], axis=1)
    score_scale = head_dim ** (-0.5)
    near_scores = (
        jnp.einsum(
            "ntkgd,nskd->nkgts",
            grouped_query,
            near_keys[..., :head_dim],
            preferred_element_type=jnp.float32,
        )
        * score_scale
    )
    sink_scores = sink_logits.reshape(value_heads, group_size)[None, :, :, None, None]
    slot_steps = jnp.arange(slot_length)
    columns = jnp.arange(window + slot_length)
    allowed = jnp.where(
        columns[None, :] < window,
        columns[None, :] > slot_steps[:, None],
        columns[None, :] - window <= slot_steps[:, None],
    )
    near_scores = jnp.where(allowed, near_scores, -jnp.inf)
    largest = jnp.maximum(jnp.max(near_scores, axis=-1, keepdims=True), sink_scores)
    near_weights = jnp.exp(near_scores - largest)
    normalizer = jnp.sum(near_weights, axis=-1, keepdims=True) + jnp.exp(sink_scores - largest)
    near_weights = (near_weights / normalizer).astype(jnp.bfloat16)
    mixed = jnp.einsum(
        "nkgts,nskd->ntkgd",
        near_weights,
        near_keys[..., head_dim:],
        preferred_element_type=jnp.float32,
    )
    return mixed.astype(jnp.bfloat16).reshape(
        peers * slot_length, value_heads * group_size * head_dim
    )


def attend_kernel(sink_ref, q_ref, kv_ref, tail_ref, o_ref):
    slot_length = q_ref.shape[1]
    window = tail_ref.shape[1]
    head_dim = kv_ref.shape[2] // 2
    heads = q_ref.shape[2] // head_dim
    scale = head_dim ** (-0.5)
    kv = kv_ref[0]
    tail = tail_ref[0]
    own_keys, own_values = kv[:, :head_dim], kv[:, head_dim:]
    tail_keys, tail_values = tail[:, :head_dim], tail[:, head_dim:]
    step = lax.broadcasted_iota(jnp.int32, (slot_length, window), 0)
    column = lax.broadcasted_iota(jnp.int32, (slot_length, window), 1)
    tail_allowed = column > step
    own_step = lax.broadcasted_iota(jnp.int32, (slot_length, slot_length), 0)
    own_column = lax.broadcasted_iota(jnp.int32, (slot_length, slot_length), 1)
    own_allowed = own_column <= own_step
    contract = (((1,), (1,)), ((), ()))
    for head in range(heads):
        query = q_ref[0, :, head * head_dim:(head + 1) * head_dim]
        tail_scores = lax.dot_general(
            query, tail_keys, contract, preferred_element_type=jnp.float32
        ) * scale
        own_scores = lax.dot_general(
            query, own_keys, contract, preferred_element_type=jnp.float32
        ) * scale
        tail_scores = jnp.where(tail_allowed, tail_scores, -jnp.inf)
        own_scores = jnp.where(own_allowed, own_scores, -jnp.inf)
        sink = sink_ref[head]
        largest = jnp.maximum(
            jnp.maximum(
                jnp.max(tail_scores, axis=1, keepdims=True),
                jnp.max(own_scores, axis=1, keepdims=True),
            ),
            sink,
        )
        tail_weights = jnp.exp(tail_scores - largest)
        own_weights = jnp.exp(own_scores - largest)
        normalizer = (
            jnp.sum(tail_weights, axis=1, keepdims=True)
            + jnp.sum(own_weights, axis=1, keepdims=True)
            + jnp.exp(sink - largest)
        )
        tail_weights = (tail_weights / normalizer).astype(jnp.bfloat16)
        own_weights = (own_weights / normalizer).astype(jnp.bfloat16)
        mixed = jnp.dot(
            tail_weights, tail_values, preferred_element_type=jnp.float32
        ) + jnp.dot(own_weights, own_values, preferred_element_type=jnp.float32)
        o_ref[0, :, head * head_dim:(head + 1) * head_dim] = mixed.astype(o_ref.dtype)


def attend_pallas(query_slots, paired_slots, tail_rows, sink_logits):
    peers, slot_length, width = query_slots.shape
    window = tail_rows.shape[1]
    pair_width = paired_slots.shape[2]
    head_dim = pair_width // 2
    heads = width // head_dim
    flops = peers * heads * 4 * slot_length * (window + slot_length) * head_dim
    moved = 2 * (2 * query_slots.size + paired_slots.size + tail_rows.size)
    return pl.pallas_call(
        attend_kernel,
        grid=(peers,),
        in_specs=[
            pl.BlockSpec(memory_space=pltpu.SMEM),
            pl.BlockSpec((1, slot_length, width), lambda n: (n, 0, 0)),
            pl.BlockSpec((1, slot_length, pair_width), lambda n: (n, 0, 0)),
            pl.BlockSpec((1, window, pair_width), lambda n: (n, 0, 0)),
        ],
        out_specs=pl.BlockSpec((1, slot_length, width), lambda n: (n, 0, 0)),
        out_shape=jax.ShapeDtypeStruct((peers, slot_length, width), jnp.bfloat16),
        cost_estimate=pl.CostEstimate(
            flops=flops,
            transcendentals=peers * heads * slot_length * (window + slot_length),
            bytes_accessed=moved,
        ),
    )(sink_logits.astype(jnp.float32), query_slots, paired_slots, tail_rows)


def fetch_prefix(attach_slots, prefix_cache, block_of_slot, window):
    total_blocks = block_of_slot.shape[0]
    block_len = prefix_cache.shape[1]
    peers = lax.axis_size("req")
    me = lax.axis_index("req")
    held_here = prefix_cache.shape[0]
    catalog = jnp.arange(total_blocks)
    home_row = jnp.sum(
        jnp.where(block_of_slot[None, :] == catalog[:, None], catalog[None, :], 0), axis=1
    )
    wanted = attach_slots[:, None] - window + jnp.arange(window)[None, :]
    block_id = wanted // block_len
    tail_store = jnp.sum(jnp.where(block_id[..., None] == catalog, home_row, 0), axis=-1)
    tail_offset = wanted - block_id * block_len
    trailing = prefix_cache.shape[2:]
    initial = jnp.zeros((attach_slots.shape[0], window) + trailing, jnp.bfloat16)
    pieces = [prefix_cache]
    for shift in range(1, peers):
        pieces.append(
            lax.ppermute(
                prefix_cache, "req", [(i, (i + shift) % peers) for i in range(peers)]
            )
        )
    shard_rows = jnp.concatenate(pieces, axis=0)
    held_blocks = shard_rows.shape[0]
    flat_rows = shard_rows.reshape((held_blocks * block_len,) + trailing)
    inside = (tail_store >= 0) & (tail_store < held_blocks)
    store = jnp.clip(tail_store, 0, held_blocks - 1)
    owner = store // held_here
    arrival = (me - owner + peers) % peers
    picked = flat_rows[(arrival * held_here + store % held_here) * block_len + tail_offset]
    return jnp.where(inside[..., None, None], picked, initial)


def local(
    suffix_tokens,
    route_lengths,
    dest_perm,
    attach_points,
    prefix_cache,
    block_of_slot,
    sink_logits,
    attn_gain,
    w_query,
    w_keyval,
    w_out,
    mlp_gain,
    w_gate,
    w_up,
    w_down,
):
    peers = lax.axis_size("req")
    splits = lax.axis_size("tp")
    request_index = lax.axis_index("req")
    tensor_index = lax.axis_index("tp")
    slot_count, slot_length, features = suffix_tokens.shape
    feature_share = features // splits
    value_heads = w_keyval.shape[1]
    head_dim = w_keyval.shape[2] // 2
    peer_ids = jnp.arange(peers)
    slot_steps = jnp.arange(slot_length)
    my_row = lax.dynamic_index_in_dim(dest_perm, request_index, 0, keepdims=False)
    attach_table = attach_points.reshape(peers, peers)
    arriving_lengths = lax.dynamic_index_in_dim(route_lengths, request_index, 0, keepdims=False)
    arriving = (dest_perm == request_index).astype(jnp.int32)
    arriving_attach = jnp.sum(attach_table * arriving, axis=1)
    send_order = jnp.sum(
        jnp.where(my_row[None, :] == peer_ids[:, None], peer_ids[None, :], 0), axis=1
    )
    run_ends = jnp.cumsum(arriving_lengths)
    starts = run_ends - arriving_lengths
    packed_ids = jnp.arange(CAP)
    source_of = jnp.sum((run_ends[None, :] <= packed_ids[:, None]).astype(jnp.int32), axis=1)
    source_hot = (source_of[:, None] == peer_ids[None, :]).astype(jnp.int32)
    token_index = packed_ids - jnp.sum(source_hot * starts[None, :], axis=1)
    positions = jnp.sum(source_hot * arriving_attach[None, :], axis=1) + token_index
    flat_index = source_of * slot_length + token_index
    slot_source = jnp.clip(starts[:, None] + slot_steps[None, :], 0, CAP - 1).reshape(-1)
    live_mask = slot_steps[None, :] < arriving_lengths[:, None]

    def to_slots(values):
        return values[slot_source].reshape((peers, slot_length) + values.shape[1:])

    tail_rows = fetch_prefix(arriving_attach, prefix_cache, block_of_slot, WINDOW)
    my_features = lax.dynamic_slice_in_dim(
        suffix_tokens, tensor_index * feature_share, feature_share, 2
    )
    landed = lax.all_to_all(
        my_features[send_order], "req", split_axis=0, concat_axis=0, tiled=True
    )
    input_part = landed.reshape(peers * slot_length, feature_share)[flat_index]
    input_rows = lax.all_gather(input_part, "tp", axis=1, tiled=True)
    row_total = input_part.shape[0]
    normed_in = norm_rows(input_rows, attn_gain)
    queries = jnp.dot(normed_in, w_query, preferred_element_type=jnp.float32).reshape(
        row_total, -1, head_dim
    )
    queries = rotate(queries, positions).astype(jnp.bfloat16)
    paired = jnp.dot(
        normed_in, w_keyval.reshape(features, -1), preferred_element_type=jnp.float32
    ).reshape(row_total, value_heads, 2 * head_dim)
    rotated = rotate(paired[..., :head_dim], positions)
    paired = jnp.concatenate([rotated, paired[..., head_dim:]], axis=-1).astype(jnp.bfloat16)
    attended = attend_pallas(
        to_slots(queries.reshape(row_total, -1)),
        to_slots(paired.reshape(row_total, -1)),
        tail_rows.reshape(peers, WINDOW, -1),
        sink_logits,
    ).reshape(peers * slot_length, -1)[flat_index]
    partial_value = jnp.dot(attended, w_out, preferred_element_type=jnp.float32)
    summed = lax.psum_scatter(
        partial_value.astype(jnp.bfloat16), "tp", scatter_dimension=1, tiled=True
    ).astype(jnp.float32)
    residual_part = (input_part.astype(jnp.float32) + summed).astype(jnp.bfloat16)
    residual = lax.all_gather(residual_part, "tp", axis=1, tiled=True)
    normed_mid = norm_rows(residual, mlp_gain)
    gate_proj = jnp.dot(normed_mid, w_gate, preferred_element_type=jnp.float32)
    up_proj = jnp.dot(normed_mid, w_up, preferred_element_type=jnp.float32)
    hidden = (jax.nn.silu(gate_proj) * up_proj).astype(jnp.bfloat16)
    down_sum = lax.psum_scatter(
        jnp.dot(hidden, w_down, preferred_element_type=jnp.float32).astype(jnp.bfloat16),
        "tp",
        scatter_dimension=1,
        tiled=True,
    ).astype(jnp.float32)
    out_rows = (residual_part.astype(jnp.float32) + down_sum).astype(jnp.bfloat16)
    out_slots = jnp.where(live_mask[..., None], to_slots(out_rows), jnp.zeros((), jnp.bfloat16))
    returned = lax.all_to_all(out_slots, "req", split_axis=0, concat_axis=0, tiled=True)
    return returned[my_row]


def solution(mesh):
    in_specs = (
        P("req", None, None),
        P(),
        P(),
        P(),
        P("req", None, "tp", None),
        P(),
        P("tp"),
        P(),
        P(None, "tp"),
        P(None, "tp", None),
        P("tp", None),
        P(),
        P(None, "tp"),
        P(None, "tp"),
        P("tp", None),
    )
    out_specs = P("req", None, "tp")
    return jax.shard_map(local, mesh=mesh, in_specs=in_specs, out_specs=out_specs, check_vma=False)
```

```python
import jax
import jax.numpy as jnp
from jax import lax
from jax.sharding import PartitionSpec as P
from jax.experimental import pallas as pl
from jax.experimental.pallas import tpu as pltpu

WINDOW = 128
CAP = 768


ROPE_BASE = 150000.0
EPSILON = 1e-05


def norm_rows(inputs, gains):
    widened = inputs.astype(jnp.float32)
    factor = lax.rsqrt(jnp.mean(widened * widened, axis=-1, keepdims=True) + EPSILON)
    return (widened * factor * gains.astype(jnp.float32)).astype(jnp.bfloat16)


def rotate(vectors, positions):
    half_dim = vectors.shape[-1] // 2
    frequency = ROPE_BASE ** (-(jnp.arange(half_dim).astype(jnp.float32) * 2.0 / vectors.shape[-1]))
    angles = positions.astype(jnp.float32)[:, None, None] * frequency
    cosine = jnp.cos(angles)
    sine_part = jnp.sin(angles)
    first_half = vectors[..., :half_dim]
    second = vectors[..., half_dim:]
    return jnp.concatenate(
        [first_half * cosine - second * sine_part, second * cosine + first_half * sine_part],
        axis=-1,
    )


def attend(query_slots, paired_slots, tail_rows, sink_logits):
    peers, slot_length = (query_slots.shape[0], query_slots.shape[1])
    value_heads = paired_slots.shape[2]
    head_dim = paired_slots.shape[3] // 2
    group_size = query_slots.shape[2] // value_heads
    window = tail_rows.shape[1]
    grouped_query = query_slots.reshape(peers, slot_length, value_heads, group_size, head_dim)
    near_keys = jnp.concatenate([tail_rows, paired_slots], axis=1)
    score_scale = head_dim ** (-0.5)
    near_scores = (
        jnp.einsum(
            "ntkgd,nskd->nkgts",
            grouped_query,
            near_keys[..., :head_dim],
            preferred_element_type=jnp.float32,
        )
        * score_scale
    )
    sink_scores = sink_logits.reshape(value_heads, group_size)[None, :, :, None, None]
    slot_steps = jnp.arange(slot_length)
    columns = jnp.arange(window + slot_length)
    allowed = jnp.where(
        columns[None, :] < window,
        columns[None, :] > slot_steps[:, None],
        columns[None, :] - window <= slot_steps[:, None],
    )
    near_scores = jnp.where(allowed, near_scores, -jnp.inf)
    largest = jnp.maximum(jnp.max(near_scores, axis=-1, keepdims=True), sink_scores)
    near_weights = jnp.exp(near_scores - largest)
    normalizer = jnp.sum(near_weights, axis=-1, keepdims=True) + jnp.exp(sink_scores - largest)
    near_weights = (near_weights / normalizer).astype(jnp.bfloat16)
    mixed = jnp.einsum(
        "nkgts,nskd->ntkgd",
        near_weights,
        near_keys[..., head_dim:],
        preferred_element_type=jnp.float32,
    )
    return mixed.astype(jnp.bfloat16).reshape(
        peers * slot_length, value_heads * group_size * head_dim
    )


def attend_kernel(sink_ref, q_ref, kv_ref, tail_ref, o_ref):
    slot_length = q_ref.shape[1]
    window = tail_ref.shape[1]
    head_dim = kv_ref.shape[2] // 2
    heads = q_ref.shape[2] // head_dim
    scale = head_dim ** (-0.5)
    kv = kv_ref[0]
    tail = tail_ref[0]
    own_keys, own_values = kv[:, :head_dim], kv[:, head_dim:]
    tail_keys, tail_values = tail[:, :head_dim], tail[:, head_dim:]
    step = lax.broadcasted_iota(jnp.int32, (slot_length, window), 0)
    column = lax.broadcasted_iota(jnp.int32, (slot_length, window), 1)
    tail_allowed = column > step
    own_step = lax.broadcasted_iota(jnp.int32, (slot_length, slot_length), 0)
    own_column = lax.broadcasted_iota(jnp.int32, (slot_length, slot_length), 1)
    own_allowed = own_column <= own_step
    contract = (((1,), (1,)), ((), ()))
    for head in range(heads):
        query = q_ref[0, :, head * head_dim:(head + 1) * head_dim]
        tail_scores = lax.dot_general(
            query, tail_keys, contract, preferred_element_type=jnp.float32
        ) * scale
        own_scores = lax.dot_general(
            query, own_keys, contract, preferred_element_type=jnp.float32
        ) * scale
        tail_scores = jnp.where(tail_allowed, tail_scores, -jnp.inf)
        own_scores = jnp.where(own_allowed, own_scores, -jnp.inf)
        sink = sink_ref[head]
        largest = jnp.maximum(
            jnp.maximum(
                jnp.max(tail_scores, axis=1, keepdims=True),
                jnp.max(own_scores, axis=1, keepdims=True),
            ),
            sink,
        )
        tail_weights = jnp.exp(tail_scores - largest)
        own_weights = jnp.exp(own_scores - largest)
        normalizer = (
            jnp.sum(tail_weights, axis=1, keepdims=True)
            + jnp.sum(own_weights, axis=1, keepdims=True)
            + jnp.exp(sink - largest)
        )
        tail_weights = (tail_weights / normalizer).astype(jnp.bfloat16)
        own_weights = (own_weights / normalizer).astype(jnp.bfloat16)
        mixed = jnp.dot(
            tail_weights, tail_values, preferred_element_type=jnp.float32
        ) + jnp.dot(own_weights, own_values, preferred_element_type=jnp.float32)
        o_ref[0, :, head * head_dim:(head + 1) * head_dim] = mixed.astype(o_ref.dtype)


def attend_pallas(query_slots, paired_slots, tail_rows, sink_logits):
    peers, slot_length, width = query_slots.shape
    window = tail_rows.shape[1]
    pair_width = paired_slots.shape[2]
    head_dim = pair_width // 2
    heads = width // head_dim
    flops = peers * heads * 4 * slot_length * (window + slot_length) * head_dim
    moved = 2 * (2 * query_slots.size + paired_slots.size + tail_rows.size)
    return pl.pallas_call(
        attend_kernel,
        grid=(peers,),
        in_specs=[
            pl.BlockSpec(memory_space=pltpu.SMEM),
            pl.BlockSpec((1, slot_length, width), lambda n: (n, 0, 0)),
            pl.BlockSpec((1, slot_length, pair_width), lambda n: (n, 0, 0)),
            pl.BlockSpec((1, window, pair_width), lambda n: (n, 0, 0)),
        ],
        out_specs=pl.BlockSpec((1, slot_length, width), lambda n: (n, 0, 0)),
        out_shape=jax.ShapeDtypeStruct((peers, slot_length, width), jnp.bfloat16),
        cost_estimate=pl.CostEstimate(
            flops=flops,
            transcendentals=peers * heads * slot_length * (window + slot_length),
            bytes_accessed=moved,
        ),
    )(sink_logits.astype(jnp.float32), query_slots, paired_slots, tail_rows)


def fetch_prefix(attach_slots, prefix_cache, block_of_slot, window):
    total_blocks = block_of_slot.shape[0]
    block_len = prefix_cache.shape[1]
    catalog = jnp.arange(total_blocks)
    home_row = jnp.sum(
        jnp.where(block_of_slot[None, :] == catalog[:, None], catalog[None, :], 0), axis=1
    )
    first_block = jnp.clip((attach_slots - window) // block_len, 0, total_blocks - 1)
    second_block = jnp.clip(first_block + 1, 0, total_blocks - 1)
    offset = attach_slots - window - first_block * block_len
    shard_rows = lax.all_gather(prefix_cache, "req", axis=0, tiled=True)
    shard_rows = shard_rows.reshape(total_blocks, block_len, -1)
    pair = jnp.stack([home_row[first_block], home_row[second_block]], axis=1)
    both = shard_rows[pair].reshape(attach_slots.shape[0], 2 * block_len, -1)
    picks = (
        jnp.arange(2 * block_len)[None, None, :]
        == offset[:, None, None] + jnp.arange(window)[None, :, None]
    ).astype(jnp.bfloat16)
    return jnp.einsum(
        "ruk,rkd->rud", picks, both, preferred_element_type=jnp.float32
    ).astype(jnp.bfloat16)


def local(
    suffix_tokens,
    route_lengths,
    dest_perm,
    attach_points,
    prefix_cache,
    block_of_slot,
    sink_logits,
    attn_gain,
    w_query,
    w_keyval,
    w_out,
    mlp_gain,
    w_gate,
    w_up,
    w_down,
):
    peers = lax.axis_size("req")
    splits = lax.axis_size("tp")
    request_index = lax.axis_index("req")
    tensor_index = lax.axis_index("tp")
    slot_count, slot_length, features = suffix_tokens.shape
    feature_share = features // splits
    value_heads = w_keyval.shape[1]
    head_dim = w_keyval.shape[2] // 2
    peer_ids = jnp.arange(peers)
    slot_steps = jnp.arange(slot_length)
    my_row = lax.dynamic_index_in_dim(dest_perm, request_index, 0, keepdims=False)
    attach_table = attach_points.reshape(peers, peers)
    arriving_lengths = lax.dynamic_index_in_dim(route_lengths, request_index, 0, keepdims=False)
    arriving = (dest_perm == request_index).astype(jnp.int32)
    arriving_attach = jnp.sum(attach_table * arriving, axis=1)
    send_order = jnp.sum(
        jnp.where(my_row[None, :] == peer_ids[:, None], peer_ids[None, :], 0), axis=1
    )
    run_ends = jnp.cumsum(arriving_lengths)
    starts = run_ends - arriving_lengths
    packed_ids = jnp.arange(CAP)
    source_of = jnp.sum((run_ends[None, :] <= packed_ids[:, None]).astype(jnp.int32), axis=1)
    source_hot = (source_of[:, None] == peer_ids[None, :]).astype(jnp.int32)
    token_index = packed_ids - jnp.sum(source_hot * starts[None, :], axis=1)
    positions = jnp.sum(source_hot * arriving_attach[None, :], axis=1) + token_index
    flat_index = source_of * slot_length + token_index
    slot_source = jnp.clip(starts[:, None] + slot_steps[None, :], 0, CAP - 1).reshape(-1)
    live_mask = slot_steps[None, :] < arriving_lengths[:, None]

    slot_pick = (
        (jnp.arange(CAP)[None, :] == slot_source[:, None]) & live_mask.reshape(-1)[:, None]
    ).astype(jnp.bfloat16)
    pack_pick = (
        jnp.arange(peers * slot_length)[None, :] == flat_index[:, None]
    ).astype(jnp.bfloat16)

    def to_slots(values):
        moved = jnp.dot(slot_pick, values, preferred_element_type=jnp.float32)
        return moved.astype(values.dtype).reshape((peers, slot_length) + values.shape[1:])

    def to_packed(values):
        return jnp.dot(pack_pick, values, preferred_element_type=jnp.float32).astype(values.dtype)

    tail_rows = fetch_prefix(arriving_attach, prefix_cache, block_of_slot, WINDOW)
    my_features = lax.dynamic_slice_in_dim(
        suffix_tokens, tensor_index * feature_share, feature_share, 2
    )
    landed = lax.all_to_all(
        my_features[send_order], "req", split_axis=0, concat_axis=0, tiled=True
    )
    input_part = to_packed(landed.reshape(peers * slot_length, feature_share))
    input_rows = lax.all_gather(input_part, "tp", axis=1, tiled=True)
    row_total = input_part.shape[0]
    normed_in = norm_rows(input_rows, attn_gain)
    queries = jnp.dot(normed_in, w_query, preferred_element_type=jnp.float32).reshape(
        row_total, -1, head_dim
    )
    queries = rotate(queries, positions).astype(jnp.bfloat16)
    paired = jnp.dot(
        normed_in, w_keyval.reshape(features, -1), preferred_element_type=jnp.float32
    ).reshape(row_total, value_heads, 2 * head_dim)
    rotated = rotate(paired[..., :head_dim], positions)
    paired = jnp.concatenate([rotated, paired[..., head_dim:]], axis=-1).astype(jnp.bfloat16)
    attended = attend_pallas(
        to_slots(queries.reshape(row_total, -1)),
        to_slots(paired.reshape(row_total, -1)),
        tail_rows,
        sink_logits,
    ).reshape(peers * slot_length, -1)
    attended = to_packed(attended)
    partial_value = jnp.dot(attended, w_out, preferred_element_type=jnp.float32)
    summed = lax.psum_scatter(
        partial_value.astype(jnp.bfloat16), "tp", scatter_dimension=1, tiled=True
    ).astype(jnp.float32)
    residual_part = (input_part.astype(jnp.float32) + summed).astype(jnp.bfloat16)
    residual = lax.all_gather(residual_part, "tp", axis=1, tiled=True)
    normed_mid = norm_rows(residual, mlp_gain)
    gate_proj = jnp.dot(normed_mid, w_gate, preferred_element_type=jnp.float32)
    up_proj = jnp.dot(normed_mid, w_up, preferred_element_type=jnp.float32)
    hidden = (jax.nn.silu(gate_proj) * up_proj).astype(jnp.bfloat16)
    down_sum = lax.psum_scatter(
        jnp.dot(hidden, w_down, preferred_element_type=jnp.float32).astype(jnp.bfloat16),
        "tp",
        scatter_dimension=1,
        tiled=True,
    ).astype(jnp.float32)
    out_rows = (residual_part.astype(jnp.float32) + down_sum).astype(jnp.bfloat16)
    out_slots = to_slots(out_rows)
    returned = lax.all_to_all(out_slots, "req", split_axis=0, concat_axis=0, tiled=True)
    return returned[my_row]


def solution(mesh):
    in_specs = (
        P("req", None, None),
        P(),
        P(),
        P(),
        P("req", None, "tp", None),
        P(),
        P("tp"),
        P(),
        P(None, "tp"),
        P(None, "tp", None),
        P("tp", None),
        P(),
        P(None, "tp"),
        P(None, "tp"),
        P("tp", None),
    )
    out_specs = P("req", None, "tp")
    return jax.shard_map(local, mesh=mesh, in_specs=in_specs, out_specs=out_specs, check_vma=False)
```

```python
import jax
import jax.numpy as jnp
from jax import lax
from jax.sharding import PartitionSpec as P
from jax.experimental import pallas as pl
from jax.experimental.pallas import tpu as pltpu

WINDOW = 128
TP = ("x", "core")
CAP = 768


ROPE_BASE = 150000.0
EPSILON = 1e-05


def norm_rows(inputs, gains):
    widened = inputs.astype(jnp.float32)
    factor = lax.rsqrt(jnp.mean(widened * widened, axis=-1, keepdims=True) + EPSILON)
    return (widened * factor * gains.astype(jnp.float32)).astype(jnp.bfloat16)


def rotate(vectors, positions):
    half_dim = vectors.shape[-1] // 2
    frequency = ROPE_BASE ** (-(jnp.arange(half_dim).astype(jnp.float32) * 2.0 / vectors.shape[-1]))
    angles = positions.astype(jnp.float32)[:, None, None] * frequency
    cosine = jnp.cos(angles)
    sine_part = jnp.sin(angles)
    first_half = vectors[..., :half_dim]
    second = vectors[..., half_dim:]
    return jnp.concatenate(
        [first_half * cosine - second * sine_part, second * cosine + first_half * sine_part],
        axis=-1,
    )


def attend(query_slots, paired_slots, tail_rows, sink_logits):
    peers, slot_length = (query_slots.shape[0], query_slots.shape[1])
    value_heads = paired_slots.shape[2]
    head_dim = paired_slots.shape[3] // 2
    group_size = query_slots.shape[2] // value_heads
    window = tail_rows.shape[1]
    grouped_query = query_slots.reshape(peers, slot_length, value_heads, group_size, head_dim)
    near_keys = jnp.concatenate([tail_rows, paired_slots], axis=1)
    score_scale = head_dim ** (-0.5)
    near_scores = (
        jnp.einsum(
            "ntkgd,nskd->nkgts",
            grouped_query,
            near_keys[..., :head_dim],
            preferred_element_type=jnp.float32,
        )
        * score_scale
    )
    sink_scores = sink_logits.reshape(value_heads, group_size)[None, :, :, None, None]
    slot_steps = jnp.arange(slot_length)
    columns = jnp.arange(window + slot_length)
    allowed = jnp.where(
        columns[None, :] < window,
        columns[None, :] > slot_steps[:, None],
        columns[None, :] - window <= slot_steps[:, None],
    )
    near_scores = jnp.where(allowed, near_scores, -jnp.inf)
    largest = jnp.maximum(jnp.max(near_scores, axis=-1, keepdims=True), sink_scores)
    near_weights = jnp.exp(near_scores - largest)
    normalizer = jnp.sum(near_weights, axis=-1, keepdims=True) + jnp.exp(sink_scores - largest)
    near_weights = (near_weights / normalizer).astype(jnp.bfloat16)
    mixed = jnp.einsum(
        "nkgts,nskd->ntkgd",
        near_weights,
        near_keys[..., head_dim:],
        preferred_element_type=jnp.float32,
    )
    return mixed.astype(jnp.bfloat16).reshape(
        peers * slot_length, value_heads * group_size * head_dim
    )


def attend_kernel(sink_ref, q_ref, kv_ref, tail_ref, o_ref):
    slot_length = q_ref.shape[1]
    window = tail_ref.shape[1]
    head_dim = kv_ref.shape[2] // 2
    heads = q_ref.shape[2] // head_dim
    scale = head_dim ** (-0.5)
    kv = kv_ref[0]
    tail = tail_ref[0]
    own_keys, own_values = kv[:, :head_dim], kv[:, head_dim:]
    tail_keys, tail_values = tail[:, :head_dim], tail[:, head_dim:]
    step = lax.broadcasted_iota(jnp.int32, (slot_length, window), 0)
    column = lax.broadcasted_iota(jnp.int32, (slot_length, window), 1)
    tail_allowed = column > step
    own_step = lax.broadcasted_iota(jnp.int32, (slot_length, slot_length), 0)
    own_column = lax.broadcasted_iota(jnp.int32, (slot_length, slot_length), 1)
    own_allowed = own_column <= own_step
    contract = (((1,), (1,)), ((), ()))
    for head in range(heads):
        query = q_ref[0, :, head * head_dim:(head + 1) * head_dim]
        tail_scores = lax.dot_general(
            query, tail_keys, contract, preferred_element_type=jnp.float32
        ) * scale
        own_scores = lax.dot_general(
            query, own_keys, contract, preferred_element_type=jnp.float32
        ) * scale
        tail_scores = jnp.where(tail_allowed, tail_scores, -jnp.inf)
        own_scores = jnp.where(own_allowed, own_scores, -jnp.inf)
        sink = sink_ref[head]
        largest = jnp.maximum(
            jnp.maximum(
                jnp.max(tail_scores, axis=1, keepdims=True),
                jnp.max(own_scores, axis=1, keepdims=True),
            ),
            sink,
        )
        tail_weights = jnp.exp(tail_scores - largest)
        own_weights = jnp.exp(own_scores - largest)
        normalizer = (
            jnp.sum(tail_weights, axis=1, keepdims=True)
            + jnp.sum(own_weights, axis=1, keepdims=True)
            + jnp.exp(sink - largest)
        )
        tail_weights = (tail_weights / normalizer).astype(jnp.bfloat16)
        own_weights = (own_weights / normalizer).astype(jnp.bfloat16)
        mixed = jnp.dot(
            tail_weights, tail_values, preferred_element_type=jnp.float32
        ) + jnp.dot(own_weights, own_values, preferred_element_type=jnp.float32)
        o_ref[0, :, head * head_dim:(head + 1) * head_dim] = mixed.astype(o_ref.dtype)


def attend_pallas(query_slots, paired_slots, tail_rows, sink_logits):
    peers, slot_length, width = query_slots.shape
    window = tail_rows.shape[1]
    pair_width = paired_slots.shape[2]
    head_dim = pair_width // 2
    heads = width // head_dim
    flops = peers * heads * 4 * slot_length * (window + slot_length) * head_dim
    moved = 2 * (2 * query_slots.size + paired_slots.size + tail_rows.size)
    return pl.pallas_call(
        attend_kernel,
        grid=(peers,),
        in_specs=[
            pl.BlockSpec(memory_space=pltpu.SMEM),
            pl.BlockSpec((1, slot_length, width), lambda n: (n, 0, 0)),
            pl.BlockSpec((1, slot_length, pair_width), lambda n: (n, 0, 0)),
            pl.BlockSpec((1, window, pair_width), lambda n: (n, 0, 0)),
        ],
        out_specs=pl.BlockSpec((1, slot_length, width), lambda n: (n, 0, 0)),
        out_shape=jax.ShapeDtypeStruct((peers, slot_length, width), jnp.bfloat16),
        cost_estimate=pl.CostEstimate(
            flops=flops,
            transcendentals=peers * heads * slot_length * (window + slot_length),
            bytes_accessed=moved,
        ),
    )(sink_logits.astype(jnp.float32), query_slots, paired_slots, tail_rows)


def fetch_prefix(attach_slots, prefix_cache, block_of_slot, window):
    total_blocks = block_of_slot.shape[0]
    block_len = prefix_cache.shape[1]
    catalog = jnp.arange(total_blocks)
    home_row = jnp.sum(
        jnp.where(block_of_slot[None, :] == catalog[:, None], catalog[None, :], 0), axis=1
    )
    first_block = jnp.clip((attach_slots - window) // block_len, 0, total_blocks - 1)
    second_block = jnp.clip(first_block + 1, 0, total_blocks - 1)
    offset = attach_slots - window - first_block * block_len
    shard_rows = lax.all_gather(prefix_cache, "req", axis=0, tiled=True)
    shard_rows = shard_rows.reshape(total_blocks, block_len, -1)
    pair = jnp.stack([home_row[first_block], home_row[second_block]], axis=1)
    both = shard_rows[pair].reshape(attach_slots.shape[0], 2 * block_len, -1)
    picks = (
        jnp.arange(2 * block_len)[None, None, :]
        == offset[:, None, None] + jnp.arange(window)[None, :, None]
    ).astype(jnp.bfloat16)
    return jnp.einsum(
        "ruk,rkd->rud", picks, both, preferred_element_type=jnp.float32
    ).astype(jnp.bfloat16)


def gather_features(part):
    chips = lax.axis_size("x")
    cores = lax.axis_size("core")
    rows, share = part.shape
    across = lax.all_gather(part, "x", axis=1, tiled=True)
    both = lax.all_gather(across, "core", axis=1, tiled=True)
    return both.reshape(rows, cores, chips, share).transpose(0, 2, 1, 3).reshape(rows, -1)


def scatter_features(whole):
    chips = lax.axis_size("x")
    cores = lax.axis_size("core")
    rows, width = whole.shape
    share = width // (chips * cores)
    ordered = whole.reshape(rows, chips, cores, share).transpose(0, 2, 1, 3).reshape(rows, -1)
    inside = lax.psum_scatter(ordered, "core", scatter_dimension=1, tiled=True)
    return lax.psum_scatter(inside, "x", scatter_dimension=1, tiled=True)


def local(
    suffix_tokens,
    route_lengths,
    dest_perm,
    attach_points,
    prefix_cache,
    block_of_slot,
    sink_logits,
    attn_gain,
    w_query,
    w_keyval,
    w_out,
    mlp_gain,
    w_gate,
    w_up,
    w_down,
):
    peers = lax.axis_size("req")
    splits = lax.axis_size(("x", "core"))
    request_index = lax.axis_index("req")
    tensor_index = lax.axis_index(("x", "core"))
    slot_count, slot_length, features = suffix_tokens.shape
    feature_share = features // splits
    value_heads = w_keyval.shape[1]
    head_dim = w_keyval.shape[2] // 2
    peer_ids = jnp.arange(peers)
    slot_steps = jnp.arange(slot_length)
    my_row = lax.dynamic_index_in_dim(dest_perm, request_index, 0, keepdims=False)
    attach_table = attach_points.reshape(peers, peers)
    arriving_lengths = lax.dynamic_index_in_dim(route_lengths, request_index, 0, keepdims=False)
    arriving = (dest_perm == request_index).astype(jnp.int32)
    arriving_attach = jnp.sum(attach_table * arriving, axis=1)
    send_order = jnp.sum(
        jnp.where(my_row[None, :] == peer_ids[:, None], peer_ids[None, :], 0), axis=1
    )
    run_ends = jnp.cumsum(arriving_lengths)
    starts = run_ends - arriving_lengths
    packed_ids = jnp.arange(CAP)
    source_of = jnp.sum((run_ends[None, :] <= packed_ids[:, None]).astype(jnp.int32), axis=1)
    source_hot = (source_of[:, None] == peer_ids[None, :]).astype(jnp.int32)
    token_index = packed_ids - jnp.sum(source_hot * starts[None, :], axis=1)
    positions = jnp.sum(source_hot * arriving_attach[None, :], axis=1) + token_index
    flat_index = source_of * slot_length + token_index
    slot_source = jnp.clip(starts[:, None] + slot_steps[None, :], 0, CAP - 1).reshape(-1)
    live_mask = slot_steps[None, :] < arriving_lengths[:, None]

    slot_pick = (
        (jnp.arange(CAP)[None, :] == slot_source[:, None]) & live_mask.reshape(-1)[:, None]
    ).astype(jnp.bfloat16)
    pack_pick = (
        jnp.arange(peers * slot_length)[None, :] == flat_index[:, None]
    ).astype(jnp.bfloat16)

    def to_slots(values):
        moved = jnp.dot(slot_pick, values, preferred_element_type=jnp.float32)
        return moved.astype(values.dtype).reshape((peers, slot_length) + values.shape[1:])

    def to_packed(values):
        return jnp.dot(pack_pick, values, preferred_element_type=jnp.float32).astype(values.dtype)

    tail_rows = fetch_prefix(arriving_attach, prefix_cache, block_of_slot, WINDOW)
    my_features = lax.dynamic_slice_in_dim(
        suffix_tokens, tensor_index * feature_share, feature_share, 2
    )
    landed = lax.all_to_all(
        my_features[send_order], "req", split_axis=0, concat_axis=0, tiled=True
    )
    input_part = to_packed(landed.reshape(peers * slot_length, feature_share))
    input_rows = gather_features(input_part)
    row_total = input_part.shape[0]
    normed_in = norm_rows(input_rows, attn_gain)
    queries = jnp.dot(normed_in, w_query, preferred_element_type=jnp.float32).reshape(
        row_total, -1, head_dim
    )
    queries = rotate(queries, positions).astype(jnp.bfloat16)
    paired = jnp.dot(
        normed_in, w_keyval.reshape(features, -1), preferred_element_type=jnp.float32
    ).reshape(row_total, value_heads, 2 * head_dim)
    rotated = rotate(paired[..., :head_dim], positions)
    paired = jnp.concatenate([rotated, paired[..., head_dim:]], axis=-1).astype(jnp.bfloat16)
    attended = attend_pallas(
        to_slots(queries.reshape(row_total, -1)),
        to_slots(paired.reshape(row_total, -1)),
        tail_rows,
        sink_logits,
    ).reshape(peers * slot_length, -1)
    attended = to_packed(attended)
    partial_value = jnp.dot(attended, w_out, preferred_element_type=jnp.float32)
    summed = scatter_features(partial_value.astype(jnp.bfloat16)).astype(jnp.float32)
    residual_part = (input_part.astype(jnp.float32) + summed).astype(jnp.bfloat16)
    residual = gather_features(residual_part)
    normed_mid = norm_rows(residual, mlp_gain)
    gate_proj = jnp.dot(normed_mid, w_gate, preferred_element_type=jnp.float32)
    up_proj = jnp.dot(normed_mid, w_up, preferred_element_type=jnp.float32)
    hidden = (jax.nn.silu(gate_proj) * up_proj).astype(jnp.bfloat16)
    down_sum = scatter_features(
        jnp.dot(hidden, w_down, preferred_element_type=jnp.float32).astype(jnp.bfloat16)
    ).astype(jnp.float32)
    out_rows = (residual_part.astype(jnp.float32) + down_sum).astype(jnp.bfloat16)
    out_slots = to_slots(out_rows)
    returned = lax.all_to_all(out_slots, "req", split_axis=0, concat_axis=0, tiled=True)
    return returned[my_row]


def solution(mesh):
    chips = mesh.shape["tp"] // 2
    split_mesh = jax.sharding.Mesh(
        mesh.devices.reshape(mesh.shape["req"], chips, 2), ("req", "x", "core")
    )
    in_specs = (
        P("req", None, None),
        P(),
        P(),
        P(),
        P("req", None, TP, None),
        P(),
        P(TP),
        P(),
        P(None, TP),
        P(None, TP, None),
        P(TP, None),
        P(),
        P(None, TP),
        P(None, TP),
        P(TP, None),
    )
    out_specs = P("req", None, TP)
    return jax.shard_map(local, mesh=split_mesh, in_specs=in_specs, out_specs=out_specs, check_vma=False)
```

```python
import jax
import jax.numpy as jnp
from jax import lax
from jax.sharding import PartitionSpec as P
from jax.experimental import pallas as pl
from jax.experimental.pallas import tpu as pltpu

WINDOW = 128
CAP = 768


ROPE_BASE = 150000.0
EPSILON = 1e-05


def norm_rows(inputs, gains):
    widened = inputs.astype(jnp.float32)
    factor = lax.rsqrt(jnp.mean(widened * widened, axis=-1, keepdims=True) + EPSILON)
    return (widened * factor * gains.astype(jnp.float32)).astype(jnp.bfloat16)


def rotate(vectors, positions):
    half_dim = vectors.shape[-1] // 2
    frequency = ROPE_BASE ** (-(jnp.arange(half_dim).astype(jnp.float32) * 2.0 / vectors.shape[-1]))
    angles = positions.astype(jnp.float32)[:, None, None] * frequency
    cosine = jnp.cos(angles)
    sine_part = jnp.sin(angles)
    first_half = vectors[..., :half_dim]
    second = vectors[..., half_dim:]
    return jnp.concatenate(
        [first_half * cosine - second * sine_part, second * cosine + first_half * sine_part],
        axis=-1,
    )


def attend(query_slots, paired_slots, tail_rows, sink_logits):
    peers, slot_length = (query_slots.shape[0], query_slots.shape[1])
    value_heads = paired_slots.shape[2]
    head_dim = paired_slots.shape[3] // 2
    group_size = query_slots.shape[2] // value_heads
    window = tail_rows.shape[1]
    grouped_query = query_slots.reshape(peers, slot_length, value_heads, group_size, head_dim)
    near_keys = jnp.concatenate([tail_rows, paired_slots], axis=1)
    score_scale = head_dim ** (-0.5)
    near_scores = (
        jnp.einsum(
            "ntkgd,nskd->nkgts",
            grouped_query,
            near_keys[..., :head_dim],
            preferred_element_type=jnp.float32,
        )
        * score_scale
    )
    sink_scores = sink_logits.reshape(value_heads, group_size)[None, :, :, None, None]
    slot_steps = jnp.arange(slot_length)
    columns = jnp.arange(window + slot_length)
    allowed = jnp.where(
        columns[None, :] < window,
        columns[None, :] > slot_steps[:, None],
        columns[None, :] - window <= slot_steps[:, None],
    )
    near_scores = jnp.where(allowed, near_scores, -jnp.inf)
    largest = jnp.maximum(jnp.max(near_scores, axis=-1, keepdims=True), sink_scores)
    near_weights = jnp.exp(near_scores - largest)
    normalizer = jnp.sum(near_weights, axis=-1, keepdims=True) + jnp.exp(sink_scores - largest)
    near_weights = (near_weights / normalizer).astype(jnp.bfloat16)
    mixed = jnp.einsum(
        "nkgts,nskd->ntkgd",
        near_weights,
        near_keys[..., head_dim:],
        preferred_element_type=jnp.float32,
    )
    return mixed.astype(jnp.bfloat16).reshape(
        peers * slot_length, value_heads * group_size * head_dim
    )


def attend_kernel(sink_ref, q_ref, kv_ref, tail_ref, o_ref):
    batch, slot_length = q_ref.shape[0], q_ref.shape[1]
    window = tail_ref.shape[1]
    head_dim = kv_ref.shape[2] // 2
    heads = q_ref.shape[2] // head_dim
    scale = head_dim ** (-0.5)
    step = lax.broadcasted_iota(jnp.int32, (slot_length, window), 0)
    column = lax.broadcasted_iota(jnp.int32, (slot_length, window), 1)
    tail_allowed = jnp.concatenate([column > step] * heads, axis=0)
    own_step = lax.broadcasted_iota(jnp.int32, (slot_length, slot_length), 0)
    own_column = lax.broadcasted_iota(jnp.int32, (slot_length, slot_length), 1)
    own_allowed = jnp.concatenate([own_column <= own_step] * heads, axis=0)
    sink = jnp.concatenate(
        [jnp.full((slot_length, 1), sink_ref[head], jnp.float32) for head in range(heads)],
        axis=0,
    )
    contract = (((1,), (1,)), ((), ()))
    for item in range(batch):
        kv = kv_ref[item]
        tail = tail_ref[item]
        query = q_ref[item]
        stacked = jnp.concatenate(
            [query[:, head * head_dim:(head + 1) * head_dim] for head in range(heads)], axis=0
        )
        tail_scores = lax.dot_general(
            stacked, tail[:, :head_dim], contract, preferred_element_type=jnp.float32
        ) * scale
        own_scores = lax.dot_general(
            stacked, kv[:, :head_dim], contract, preferred_element_type=jnp.float32
        ) * scale
        tail_scores = jnp.where(tail_allowed, tail_scores, -jnp.inf)
        own_scores = jnp.where(own_allowed, own_scores, -jnp.inf)
        largest = jnp.maximum(
            jnp.maximum(
                jnp.max(tail_scores, axis=1, keepdims=True),
                jnp.max(own_scores, axis=1, keepdims=True),
            ),
            sink,
        )
        tail_weights = jnp.exp(tail_scores - largest)
        own_weights = jnp.exp(own_scores - largest)
        normalizer = (
            jnp.sum(tail_weights, axis=1, keepdims=True)
            + jnp.sum(own_weights, axis=1, keepdims=True)
            + jnp.exp(sink - largest)
        )
        tail_weights = (tail_weights / normalizer).astype(jnp.bfloat16)
        own_weights = (own_weights / normalizer).astype(jnp.bfloat16)
        mixed = jnp.dot(
            tail_weights, tail[:, head_dim:], preferred_element_type=jnp.float32
        ) + jnp.dot(own_weights, kv[:, head_dim:], preferred_element_type=jnp.float32)
        mixed = mixed.astype(o_ref.dtype)
        for head in range(heads):
            o_ref[item, :, head * head_dim:(head + 1) * head_dim] = mixed[
                head * slot_length:(head + 1) * slot_length
            ]


def attend_pallas(query_slots, paired_slots, tail_rows, sink_logits, batch=2):
    peers, slot_length, width = query_slots.shape
    window = tail_rows.shape[1]
    pair_width = paired_slots.shape[2]
    head_dim = pair_width // 2
    heads = width // head_dim
    flops = peers * heads * 4 * slot_length * (window + slot_length) * head_dim
    moved = 2 * (2 * query_slots.size + paired_slots.size + tail_rows.size)
    return pl.pallas_call(
        attend_kernel,
        grid=(peers // batch,),
        in_specs=[
            pl.BlockSpec(memory_space=pltpu.SMEM),
            pl.BlockSpec((batch, slot_length, width), lambda n: (n, 0, 0)),
            pl.BlockSpec((batch, slot_length, pair_width), lambda n: (n, 0, 0)),
            pl.BlockSpec((batch, window, pair_width), lambda n: (n, 0, 0)),
        ],
        out_specs=pl.BlockSpec((batch, slot_length, width), lambda n: (n, 0, 0)),
        out_shape=jax.ShapeDtypeStruct((peers, slot_length, width), jnp.bfloat16),
        cost_estimate=pl.CostEstimate(
            flops=flops,
            transcendentals=peers * heads * slot_length * (window + slot_length),
            bytes_accessed=moved,
        ),
    )(sink_logits.astype(jnp.float32), query_slots, paired_slots, tail_rows)


def fetch_prefix(attach_slots, prefix_cache, block_of_slot, window):
    total_blocks = block_of_slot.shape[0]
    block_len = prefix_cache.shape[1]
    catalog = jnp.arange(total_blocks)
    home_row = jnp.sum(
        jnp.where(block_of_slot[None, :] == catalog[:, None], catalog[None, :], 0), axis=1
    )
    first_block = jnp.clip((attach_slots - window) // block_len, 0, total_blocks - 1)
    second_block = jnp.clip(first_block + 1, 0, total_blocks - 1)
    offset = attach_slots - window - first_block * block_len
    shard_rows = lax.all_gather(prefix_cache, "req", axis=0, tiled=True)
    shard_rows = shard_rows.reshape(total_blocks, block_len, -1)
    pair = jnp.stack([home_row[first_block], home_row[second_block]], axis=1)
    both = shard_rows[pair].reshape(attach_slots.shape[0], 2 * block_len, -1)
    picks = (
        jnp.arange(2 * block_len)[None, None, :]
        == offset[:, None, None] + jnp.arange(window)[None, :, None]
    ).astype(jnp.bfloat16)
    return jnp.einsum(
        "ruk,rkd->rud", picks, both, preferred_element_type=jnp.float32
    ).astype(jnp.bfloat16)


def local(
    suffix_tokens,
    route_lengths,
    dest_perm,
    attach_points,
    prefix_cache,
    block_of_slot,
    sink_logits,
    attn_gain,
    w_query,
    w_keyval,
    w_out,
    mlp_gain,
    w_gate,
    w_up,
    w_down,
):
    peers = lax.axis_size("req")
    splits = lax.axis_size("tp")
    request_index = lax.axis_index("req")
    tensor_index = lax.axis_index("tp")
    slot_count, slot_length, features = suffix_tokens.shape
    feature_share = features // splits
    value_heads = w_keyval.shape[1]
    head_dim = w_keyval.shape[2] // 2
    peer_ids = jnp.arange(peers)
    slot_steps = jnp.arange(slot_length)
    my_row = lax.dynamic_index_in_dim(dest_perm, request_index, 0, keepdims=False)
    attach_table = attach_points.reshape(peers, peers)
    arriving_lengths = lax.dynamic_index_in_dim(route_lengths, request_index, 0, keepdims=False)
    arriving = (dest_perm == request_index).astype(jnp.int32)
    arriving_attach = jnp.sum(attach_table * arriving, axis=1)
    send_order = jnp.sum(
        jnp.where(my_row[None, :] == peer_ids[:, None], peer_ids[None, :], 0), axis=1
    )
    run_ends = jnp.cumsum(arriving_lengths)
    starts = run_ends - arriving_lengths
    packed_ids = jnp.arange(CAP)
    source_of = jnp.sum((run_ends[None, :] <= packed_ids[:, None]).astype(jnp.int32), axis=1)
    source_hot = (source_of[:, None] == peer_ids[None, :]).astype(jnp.int32)
    token_index = packed_ids - jnp.sum(source_hot * starts[None, :], axis=1)
    positions = jnp.sum(source_hot * arriving_attach[None, :], axis=1) + token_index
    flat_index = source_of * slot_length + token_index
    slot_source = jnp.clip(starts[:, None] + slot_steps[None, :], 0, CAP - 1).reshape(-1)
    live_mask = slot_steps[None, :] < arriving_lengths[:, None]

    slot_pick = (
        (jnp.arange(CAP)[None, :] == slot_source[:, None]) & live_mask.reshape(-1)[:, None]
    ).astype(jnp.bfloat16)
    pack_pick = (
        jnp.arange(peers * slot_length)[None, :] == flat_index[:, None]
    ).astype(jnp.bfloat16)

    def to_slots(values):
        moved = jnp.dot(slot_pick, values, preferred_element_type=jnp.float32)
        return moved.astype(values.dtype).reshape((peers, slot_length) + values.shape[1:])

    def to_packed(values):
        return jnp.dot(pack_pick, values, preferred_element_type=jnp.float32).astype(values.dtype)

    tail_rows = fetch_prefix(arriving_attach, prefix_cache, block_of_slot, WINDOW)
    my_features = lax.dynamic_slice_in_dim(
        suffix_tokens, tensor_index * feature_share, feature_share, 2
    )
    landed = lax.all_to_all(
        my_features[send_order], "req", split_axis=0, concat_axis=0, tiled=True
    )
    input_part = to_packed(landed.reshape(peers * slot_length, feature_share))
    input_rows = lax.all_gather(input_part, "tp", axis=1, tiled=True)
    row_total = input_part.shape[0]
    normed_in = norm_rows(input_rows, attn_gain)
    queries = jnp.dot(normed_in, w_query, preferred_element_type=jnp.float32).reshape(
        row_total, -1, head_dim
    )
    queries = rotate(queries, positions).astype(jnp.bfloat16)
    paired = jnp.dot(
        normed_in, w_keyval.reshape(features, -1), preferred_element_type=jnp.float32
    ).reshape(row_total, value_heads, 2 * head_dim)
    rotated = rotate(paired[..., :head_dim], positions)
    paired = jnp.concatenate([rotated, paired[..., head_dim:]], axis=-1).astype(jnp.bfloat16)
    attended = attend_pallas(
        to_slots(queries.reshape(row_total, -1)),
        to_slots(paired.reshape(row_total, -1)),
        tail_rows,
        sink_logits,
    ).reshape(peers * slot_length, -1)
    attended = to_packed(attended)
    partial_value = jnp.dot(attended, w_out, preferred_element_type=jnp.float32)
    summed = lax.psum_scatter(
        partial_value.astype(jnp.bfloat16), "tp", scatter_dimension=1, tiled=True
    ).astype(jnp.float32)
    residual_part = (input_part.astype(jnp.float32) + summed).astype(jnp.bfloat16)
    residual = lax.all_gather(residual_part, "tp", axis=1, tiled=True)
    normed_mid = norm_rows(residual, mlp_gain)
    gate_proj = jnp.dot(normed_mid, w_gate, preferred_element_type=jnp.float32)
    up_proj = jnp.dot(normed_mid, w_up, preferred_element_type=jnp.float32)
    hidden = (jax.nn.silu(gate_proj) * up_proj).astype(jnp.bfloat16)
    down_sum = lax.psum_scatter(
        jnp.dot(hidden, w_down, preferred_element_type=jnp.float32).astype(jnp.bfloat16),
        "tp",
        scatter_dimension=1,
        tiled=True,
    ).astype(jnp.float32)
    out_rows = (residual_part.astype(jnp.float32) + down_sum).astype(jnp.bfloat16)
    out_slots = to_slots(out_rows)
    returned = lax.all_to_all(out_slots, "req", split_axis=0, concat_axis=0, tiled=True)
    return returned[my_row]


def solution(mesh):
    in_specs = (
        P("req", None, None),
        P(),
        P(),
        P(),
        P("req", None, "tp", None),
        P(),
        P("tp"),
        P(),
        P(None, "tp"),
        P(None, "tp", None),
        P("tp", None),
        P(),
        P(None, "tp"),
        P(None, "tp"),
        P("tp", None),
    )
    out_specs = P("req", None, "tp")
    return jax.shard_map(local, mesh=mesh, in_specs=in_specs, out_specs=out_specs, check_vma=False)
```

```python
import jax
import jax.numpy as jnp
from jax import lax
from jax.sharding import PartitionSpec as P
from jax.experimental import pallas as pl
from jax.experimental.pallas import tpu as pltpu

WINDOW = 128
CAP = 768


ROPE_BASE = 150000.0
EPSILON = 1e-05


def norm_rows(inputs, gains):
    widened = inputs.astype(jnp.float32)
    factor = lax.rsqrt(jnp.mean(widened * widened, axis=-1, keepdims=True) + EPSILON)
    return (widened * factor * gains.astype(jnp.float32)).astype(jnp.bfloat16)


def rotate(vectors, positions):
    half_dim = vectors.shape[-1] // 2
    frequency = ROPE_BASE ** (-(jnp.arange(half_dim).astype(jnp.float32) * 2.0 / vectors.shape[-1]))
    angles = positions.astype(jnp.float32)[:, None, None] * frequency
    cosine = jnp.cos(angles)
    sine_part = jnp.sin(angles)
    first_half = vectors[..., :half_dim]
    second = vectors[..., half_dim:]
    return jnp.concatenate(
        [first_half * cosine - second * sine_part, second * cosine + first_half * sine_part],
        axis=-1,
    )


def attend(query_slots, paired_slots, tail_rows, sink_logits):
    peers, slot_length = (query_slots.shape[0], query_slots.shape[1])
    value_heads = paired_slots.shape[2]
    head_dim = paired_slots.shape[3] // 2
    group_size = query_slots.shape[2] // value_heads
    window = tail_rows.shape[1]
    grouped_query = query_slots.reshape(peers, slot_length, value_heads, group_size, head_dim)
    near_keys = jnp.concatenate([tail_rows, paired_slots], axis=1)
    score_scale = head_dim ** (-0.5)
    near_scores = (
        jnp.einsum(
            "ntkgd,nskd->nkgts",
            grouped_query,
            near_keys[..., :head_dim],
            preferred_element_type=jnp.float32,
        )
        * score_scale
    )
    sink_scores = sink_logits.reshape(value_heads, group_size)[None, :, :, None, None]
    slot_steps = jnp.arange(slot_length)
    columns = jnp.arange(window + slot_length)
    allowed = jnp.where(
        columns[None, :] < window,
        columns[None, :] > slot_steps[:, None],
        columns[None, :] - window <= slot_steps[:, None],
    )
    near_scores = jnp.where(allowed, near_scores, -jnp.inf)
    largest = jnp.maximum(jnp.max(near_scores, axis=-1, keepdims=True), sink_scores)
    near_weights = jnp.exp(near_scores - largest)
    normalizer = jnp.sum(near_weights, axis=-1, keepdims=True) + jnp.exp(sink_scores - largest)
    near_weights = (near_weights / normalizer).astype(jnp.bfloat16)
    mixed = jnp.einsum(
        "nkgts,nskd->ntkgd",
        near_weights,
        near_keys[..., head_dim:],
        preferred_element_type=jnp.float32,
    )
    return mixed.astype(jnp.bfloat16).reshape(
        peers * slot_length, value_heads * group_size * head_dim
    )


def attend_kernel(sink_ref, q_ref, kv_ref, tail_ref, o_ref):
    batch, slot_length = q_ref.shape[0], q_ref.shape[1]
    window = tail_ref.shape[1]
    head_dim = kv_ref.shape[2] // 2
    heads = q_ref.shape[2] // head_dim
    scale = head_dim ** (-0.5)
    step = lax.broadcasted_iota(jnp.int32, (slot_length, window), 0)
    column = lax.broadcasted_iota(jnp.int32, (slot_length, window), 1)
    tail_allowed = jnp.concatenate([column > step] * heads, axis=0)
    own_step = lax.broadcasted_iota(jnp.int32, (slot_length, slot_length), 0)
    own_column = lax.broadcasted_iota(jnp.int32, (slot_length, slot_length), 1)
    own_allowed = jnp.concatenate([own_column <= own_step] * heads, axis=0)
    sink = jnp.concatenate(
        [jnp.full((slot_length, 1), sink_ref[head], jnp.float32) for head in range(heads)],
        axis=0,
    )
    contract = (((1,), (1,)), ((), ()))
    for item in range(batch):
        kv = kv_ref[item]
        tail = tail_ref[item]
        query = q_ref[item]
        stacked = jnp.concatenate(
            [query[:, head * head_dim:(head + 1) * head_dim] for head in range(heads)], axis=0
        )
        tail_scores = lax.dot_general(
            stacked, tail[:, :head_dim], contract, preferred_element_type=jnp.float32
        ) * scale
        own_scores = lax.dot_general(
            stacked, kv[:, :head_dim], contract, preferred_element_type=jnp.float32
        ) * scale
        tail_scores = jnp.where(tail_allowed, tail_scores, -jnp.inf)
        own_scores = jnp.where(own_allowed, own_scores, -jnp.inf)
        largest = jnp.maximum(
            jnp.maximum(
                jnp.max(tail_scores, axis=1, keepdims=True),
                jnp.max(own_scores, axis=1, keepdims=True),
            ),
            sink,
        )
        tail_weights = jnp.exp(tail_scores - largest)
        own_weights = jnp.exp(own_scores - largest)
        normalizer = (
            jnp.sum(tail_weights, axis=1, keepdims=True)
            + jnp.sum(own_weights, axis=1, keepdims=True)
            + jnp.exp(sink - largest)
        )
        inverse = 1.0 / normalizer
        tail_weights = (tail_weights * inverse).astype(jnp.bfloat16)
        own_weights = (own_weights * inverse).astype(jnp.bfloat16)
        mixed = jnp.dot(
            tail_weights, tail[:, head_dim:], preferred_element_type=jnp.float32
        ) + jnp.dot(own_weights, kv[:, head_dim:], preferred_element_type=jnp.float32)
        mixed = mixed.astype(o_ref.dtype)
        for head in range(heads):
            o_ref[item, :, head * head_dim:(head + 1) * head_dim] = mixed[
                head * slot_length:(head + 1) * slot_length
            ]


def attend_pallas(query_slots, paired_slots, tail_rows, sink_logits, batch=2):
    peers, slot_length, width = query_slots.shape
    window = tail_rows.shape[1]
    pair_width = paired_slots.shape[2]
    head_dim = pair_width // 2
    heads = width // head_dim
    flops = peers * heads * 4 * slot_length * (window + slot_length) * head_dim
    moved = 2 * (2 * query_slots.size + paired_slots.size + tail_rows.size)
    return pl.pallas_call(
        attend_kernel,
        grid=(peers // batch,),
        in_specs=[
            pl.BlockSpec(memory_space=pltpu.SMEM),
            pl.BlockSpec((batch, slot_length, width), lambda n: (n, 0, 0)),
            pl.BlockSpec((batch, slot_length, pair_width), lambda n: (n, 0, 0)),
            pl.BlockSpec((batch, window, pair_width), lambda n: (n, 0, 0)),
        ],
        out_specs=pl.BlockSpec((batch, slot_length, width), lambda n: (n, 0, 0)),
        out_shape=jax.ShapeDtypeStruct((peers, slot_length, width), jnp.bfloat16),
        cost_estimate=pl.CostEstimate(
            flops=flops,
            transcendentals=peers * heads * slot_length * (window + slot_length),
            bytes_accessed=moved,
        ),
    )(sink_logits.astype(jnp.float32), query_slots, paired_slots, tail_rows)


def fetch_prefix(attach_slots, prefix_cache, block_of_slot, window):
    total_blocks = block_of_slot.shape[0]
    block_len = prefix_cache.shape[1]
    catalog = jnp.arange(total_blocks)
    home_row = jnp.sum(
        jnp.where(block_of_slot[None, :] == catalog[:, None], catalog[None, :], 0), axis=1
    )
    first_block = jnp.clip((attach_slots - window) // block_len, 0, total_blocks - 1)
    second_block = jnp.clip(first_block + 1, 0, total_blocks - 1)
    offset = attach_slots - window - first_block * block_len
    shard_rows = lax.all_gather(prefix_cache, "req", axis=0, tiled=True)
    shard_rows = shard_rows.reshape(total_blocks, block_len, -1)
    pair = jnp.stack([home_row[first_block], home_row[second_block]], axis=1)
    both = shard_rows[pair].reshape(attach_slots.shape[0], 2 * block_len, -1)
    picks = (
        jnp.arange(2 * block_len)[None, None, :]
        == offset[:, None, None] + jnp.arange(window)[None, :, None]
    ).astype(jnp.bfloat16)
    return jnp.einsum(
        "ruk,rkd->rud", picks, both, preferred_element_type=jnp.float32
    ).astype(jnp.bfloat16)


def local(
    suffix_tokens,
    route_lengths,
    dest_perm,
    attach_points,
    prefix_cache,
    block_of_slot,
    sink_logits,
    attn_gain,
    w_query,
    w_keyval,
    w_out,
    mlp_gain,
    w_gate,
    w_up,
    w_down,
):
    peers = lax.axis_size("req")
    splits = lax.axis_size("tp")
    request_index = lax.axis_index("req")
    tensor_index = lax.axis_index("tp")
    slot_count, slot_length, features = suffix_tokens.shape
    feature_share = features // splits
    value_heads = w_keyval.shape[1]
    head_dim = w_keyval.shape[2] // 2
    peer_ids = jnp.arange(peers)
    slot_steps = jnp.arange(slot_length)
    my_row = lax.dynamic_index_in_dim(dest_perm, request_index, 0, keepdims=False)
    attach_table = attach_points.reshape(peers, peers)
    arriving_lengths = lax.dynamic_index_in_dim(route_lengths, request_index, 0, keepdims=False)
    arriving = (dest_perm == request_index).astype(jnp.int32)
    arriving_attach = jnp.sum(attach_table * arriving, axis=1)
    send_order = jnp.sum(
        jnp.where(my_row[None, :] == peer_ids[:, None], peer_ids[None, :], 0), axis=1
    )
    run_ends = jnp.cumsum(arriving_lengths)
    starts = run_ends - arriving_lengths
    packed_ids = jnp.arange(CAP)
    source_of = jnp.sum((run_ends[None, :] <= packed_ids[:, None]).astype(jnp.int32), axis=1)
    source_hot = (source_of[:, None] == peer_ids[None, :]).astype(jnp.int32)
    token_index = packed_ids - jnp.sum(source_hot * starts[None, :], axis=1)
    positions = jnp.sum(source_hot * arriving_attach[None, :], axis=1) + token_index
    flat_index = source_of * slot_length + token_index
    slot_source = jnp.clip(starts[:, None] + slot_steps[None, :], 0, CAP - 1).reshape(-1)
    live_mask = slot_steps[None, :] < arriving_lengths[:, None]

    slot_pick = (
        (jnp.arange(CAP)[None, :] == slot_source[:, None]) & live_mask.reshape(-1)[:, None]
    ).astype(jnp.bfloat16)
    pack_pick = (
        jnp.arange(peers * slot_length)[None, :] == flat_index[:, None]
    ).astype(jnp.bfloat16)

    def to_slots(values):
        moved = jnp.dot(slot_pick, values, preferred_element_type=jnp.float32)
        return moved.astype(values.dtype).reshape((peers, slot_length) + values.shape[1:])

    def to_packed(values):
        return jnp.dot(pack_pick, values, preferred_element_type=jnp.float32).astype(values.dtype)

    tail_rows = fetch_prefix(arriving_attach, prefix_cache, block_of_slot, WINDOW)
    my_features = lax.dynamic_slice_in_dim(
        suffix_tokens, tensor_index * feature_share, feature_share, 2
    )
    landed = lax.all_to_all(
        my_features[send_order], "req", split_axis=0, concat_axis=0, tiled=True
    )
    input_part = to_packed(landed.reshape(peers * slot_length, feature_share))
    input_rows = lax.all_gather(input_part, "tp", axis=1, tiled=True)
    row_total = input_part.shape[0]
    normed_in = norm_rows(input_rows, attn_gain)
    queries = jnp.dot(normed_in, w_query, preferred_element_type=jnp.float32).reshape(
        row_total, -1, head_dim
    )
    queries = rotate(queries, positions).astype(jnp.bfloat16)
    paired = jnp.dot(
        normed_in, w_keyval.reshape(features, -1), preferred_element_type=jnp.float32
    ).reshape(row_total, value_heads, 2 * head_dim)
    rotated = rotate(paired[..., :head_dim], positions)
    paired = jnp.concatenate([rotated, paired[..., head_dim:]], axis=-1).astype(jnp.bfloat16)
    attended = attend_pallas(
        to_slots(queries.reshape(row_total, -1)),
        to_slots(paired.reshape(row_total, -1)),
        tail_rows,
        sink_logits,
    ).reshape(peers * slot_length, -1)
    attended = to_packed(attended)
    partial_value = jnp.dot(attended, w_out, preferred_element_type=jnp.float32)
    summed = lax.psum_scatter(
        partial_value.astype(jnp.bfloat16), "tp", scatter_dimension=1, tiled=True
    ).astype(jnp.float32)
    residual_part = (input_part.astype(jnp.float32) + summed).astype(jnp.bfloat16)
    residual = lax.all_gather(residual_part, "tp", axis=1, tiled=True)
    normed_mid = norm_rows(residual, mlp_gain)
    gate_proj = jnp.dot(normed_mid, w_gate, preferred_element_type=jnp.float32)
    up_proj = jnp.dot(normed_mid, w_up, preferred_element_type=jnp.float32)
    hidden = (jax.nn.silu(gate_proj) * up_proj).astype(jnp.bfloat16)
    down_sum = lax.psum_scatter(
        jnp.dot(hidden, w_down, preferred_element_type=jnp.float32).astype(jnp.bfloat16),
        "tp",
        scatter_dimension=1,
        tiled=True,
    ).astype(jnp.float32)
    out_rows = (residual_part.astype(jnp.float32) + down_sum).astype(jnp.bfloat16)
    out_slots = to_slots(out_rows)
    returned = lax.all_to_all(out_slots, "req", split_axis=0, concat_axis=0, tiled=True)
    return returned[my_row]


def solution(mesh):
    in_specs = (
        P("req", None, None),
        P(),
        P(),
        P(),
        P("req", None, "tp", None),
        P(),
        P("tp"),
        P(),
        P(None, "tp"),
        P(None, "tp", None),
        P("tp", None),
        P(),
        P(None, "tp"),
        P(None, "tp"),
        P("tp", None),
    )
    out_specs = P("req", None, "tp")
    return jax.shard_map(local, mesh=mesh, in_specs=in_specs, out_specs=out_specs, check_vma=False)
```

```python
import jax
import jax.numpy as jnp
from jax import lax
from jax.sharding import PartitionSpec as P
from jax.experimental import pallas as pl
from jax.experimental.pallas import tpu as pltpu

WINDOW = 128
CAP = 768


ROPE_BASE = 150000.0
EPSILON = 1e-05


def norm_rows(inputs, gains):
    widened = inputs.astype(jnp.float32)
    factor = lax.rsqrt(jnp.mean(widened * widened, axis=-1, keepdims=True) + EPSILON)
    return (widened * factor * gains.astype(jnp.float32)).astype(jnp.bfloat16)


def rotate(vectors, positions):
    half_dim = vectors.shape[-1] // 2
    frequency = ROPE_BASE ** (-(jnp.arange(half_dim).astype(jnp.float32) * 2.0 / vectors.shape[-1]))
    angles = positions.astype(jnp.float32)[:, None, None] * frequency
    cosine = jnp.cos(angles)
    sine_part = jnp.sin(angles)
    first_half = vectors[..., :half_dim]
    second = vectors[..., half_dim:]
    return jnp.concatenate(
        [first_half * cosine - second * sine_part, second * cosine + first_half * sine_part],
        axis=-1,
    )


def attend(query_slots, paired_slots, tail_rows, sink_logits):
    peers, slot_length = (query_slots.shape[0], query_slots.shape[1])
    value_heads = paired_slots.shape[2]
    head_dim = paired_slots.shape[3] // 2
    group_size = query_slots.shape[2] // value_heads
    window = tail_rows.shape[1]
    grouped_query = query_slots.reshape(peers, slot_length, value_heads, group_size, head_dim)
    near_keys = jnp.concatenate([tail_rows, paired_slots], axis=1)
    score_scale = head_dim ** (-0.5)
    near_scores = (
        jnp.einsum(
            "ntkgd,nskd->nkgts",
            grouped_query,
            near_keys[..., :head_dim],
            preferred_element_type=jnp.float32,
        )
        * score_scale
    )
    sink_scores = sink_logits.reshape(value_heads, group_size)[None, :, :, None, None]
    slot_steps = jnp.arange(slot_length)
    columns = jnp.arange(window + slot_length)
    allowed = jnp.where(
        columns[None, :] < window,
        columns[None, :] > slot_steps[:, None],
        columns[None, :] - window <= slot_steps[:, None],
    )
    near_scores = jnp.where(allowed, near_scores, -jnp.inf)
    largest = jnp.maximum(jnp.max(near_scores, axis=-1, keepdims=True), sink_scores)
    near_weights = jnp.exp(near_scores - largest)
    normalizer = jnp.sum(near_weights, axis=-1, keepdims=True) + jnp.exp(sink_scores - largest)
    near_weights = (near_weights / normalizer).astype(jnp.bfloat16)
    mixed = jnp.einsum(
        "nkgts,nskd->ntkgd",
        near_weights,
        near_keys[..., head_dim:],
        preferred_element_type=jnp.float32,
    )
    return mixed.astype(jnp.bfloat16).reshape(
        peers * slot_length, value_heads * group_size * head_dim
    )


def attend_kernel(sink_ref, q_ref, kv_ref, tail_ref, o_ref):
    batch, slot_length = q_ref.shape[0], q_ref.shape[1]
    window = tail_ref.shape[1]
    head_dim = kv_ref.shape[2] // 2
    heads = q_ref.shape[2] // head_dim
    scale = head_dim ** (-0.5)
    step = lax.broadcasted_iota(jnp.int32, (slot_length, window), 0)
    column = lax.broadcasted_iota(jnp.int32, (slot_length, window), 1)
    tail_allowed = jnp.concatenate([column > step] * heads, axis=0)
    own_step = lax.broadcasted_iota(jnp.int32, (slot_length, slot_length), 0)
    own_column = lax.broadcasted_iota(jnp.int32, (slot_length, slot_length), 1)
    own_allowed = jnp.concatenate([own_column <= own_step] * heads, axis=0)
    sink = jnp.concatenate(
        [jnp.full((slot_length, 1), sink_ref[head], jnp.float32) for head in range(heads)],
        axis=0,
    )
    contract = (((1,), (1,)), ((), ()))
    for item in range(batch):
        kv = kv_ref[item]
        tail = tail_ref[item]
        query = q_ref[item]
        stacked = jnp.concatenate(
            [query[:, head * head_dim:(head + 1) * head_dim] for head in range(heads)], axis=0
        )
        tail_scores = lax.dot_general(
            stacked, tail[:, :head_dim], contract, preferred_element_type=jnp.float32
        ) * scale
        own_scores = lax.dot_general(
            stacked, kv[:, :head_dim], contract, preferred_element_type=jnp.float32
        ) * scale
        tail_scores = jnp.where(tail_allowed, tail_scores, -jnp.inf)
        own_scores = jnp.where(own_allowed, own_scores, -jnp.inf)
        largest = jnp.maximum(
            jnp.maximum(
                jnp.max(tail_scores, axis=1, keepdims=True),
                jnp.max(own_scores, axis=1, keepdims=True),
            ),
            sink,
        )
        tail_weights = jnp.exp(tail_scores - largest)
        own_weights = jnp.exp(own_scores - largest)
        normalizer = (
            jnp.sum(tail_weights, axis=1, keepdims=True)
            + jnp.sum(own_weights, axis=1, keepdims=True)
            + jnp.exp(sink - largest)
        )
        inverse = 1.0 / normalizer
        tail_weights = (tail_weights * inverse).astype(jnp.bfloat16)
        own_weights = (own_weights * inverse).astype(jnp.bfloat16)
        mixed = jnp.dot(
            tail_weights, tail[:, head_dim:], preferred_element_type=jnp.float32
        ) + jnp.dot(own_weights, kv[:, head_dim:], preferred_element_type=jnp.float32)
        mixed = mixed.astype(o_ref.dtype)
        for head in range(heads):
            o_ref[item, :, head * head_dim:(head + 1) * head_dim] = mixed[
                head * slot_length:(head + 1) * slot_length
            ]


def attend_pallas(query_slots, paired_slots, tail_rows, sink_logits, batch=2):
    peers, slot_length, width = query_slots.shape
    window = tail_rows.shape[1]
    pair_width = paired_slots.shape[2]
    head_dim = pair_width // 2
    heads = width // head_dim
    flops = peers * heads * 4 * slot_length * (window + slot_length) * head_dim
    moved = 2 * (2 * query_slots.size + paired_slots.size + tail_rows.size)
    return pl.pallas_call(
        attend_kernel,
        grid=(peers // batch,),
        in_specs=[
            pl.BlockSpec(memory_space=pltpu.SMEM),
            pl.BlockSpec((batch, slot_length, width), lambda n: (n, 0, 0)),
            pl.BlockSpec((batch, slot_length, pair_width), lambda n: (n, 0, 0)),
            pl.BlockSpec((batch, window, pair_width), lambda n: (n, 0, 0)),
        ],
        out_specs=pl.BlockSpec((batch, slot_length, width), lambda n: (n, 0, 0)),
        out_shape=jax.ShapeDtypeStruct((peers, slot_length, width), jnp.bfloat16),
        cost_estimate=pl.CostEstimate(
            flops=flops,
            transcendentals=peers * heads * slot_length * (window + slot_length),
            bytes_accessed=moved,
        ),
    )(sink_logits.astype(jnp.float32), query_slots, paired_slots, tail_rows)


def fetch_prefix(attach_slots, prefix_cache, block_of_slot, window):
    total_blocks = block_of_slot.shape[0]
    block_len = prefix_cache.shape[1]
    catalog = jnp.arange(total_blocks)
    home_row = jnp.sum(
        jnp.where(block_of_slot[None, :] == catalog[:, None], catalog[None, :], 0), axis=1
    )
    first_block = jnp.clip((attach_slots - window) // block_len, 0, total_blocks - 1)
    second_block = jnp.clip(first_block + 1, 0, total_blocks - 1)
    offset = attach_slots - window - first_block * block_len
    shard_rows = lax.all_gather(prefix_cache, "req", axis=0, tiled=True)
    shard_rows = shard_rows.reshape(total_blocks, block_len, -1)
    pair = jnp.stack([home_row[first_block], home_row[second_block]], axis=1)
    both = shard_rows[pair].reshape(attach_slots.shape[0], 2 * block_len, -1)
    picks = (
        jnp.arange(2 * block_len)[None, None, :]
        == offset[:, None, None] + jnp.arange(window)[None, :, None]
    ).astype(jnp.bfloat16)
    return jnp.einsum(
        "ruk,rkd->rud", picks, both, preferred_element_type=jnp.float32
    ).astype(jnp.bfloat16)


def local(
    suffix_tokens,
    route_lengths,
    dest_perm,
    attach_points,
    prefix_cache,
    block_of_slot,
    sink_logits,
    attn_gain,
    w_query,
    w_keyval,
    w_out,
    mlp_gain,
    w_gate,
    w_up,
    w_down,
):
    peers = lax.axis_size("req")
    splits = lax.axis_size("tp")
    request_index = lax.axis_index("req")
    tensor_index = lax.axis_index("tp")
    slot_count, slot_length, features = suffix_tokens.shape
    feature_share = features // splits
    value_heads = w_keyval.shape[1]
    head_dim = w_keyval.shape[2] // 2
    peer_ids = jnp.arange(peers)
    slot_steps = jnp.arange(slot_length)
    my_row = lax.dynamic_index_in_dim(dest_perm, request_index, 0, keepdims=False)
    attach_table = attach_points.reshape(peers, peers)
    arriving_lengths = lax.dynamic_index_in_dim(route_lengths, request_index, 0, keepdims=False)
    arriving = (dest_perm == request_index).astype(jnp.int32)
    arriving_attach = jnp.sum(attach_table * arriving, axis=1)
    send_order = jnp.sum(
        jnp.where(my_row[None, :] == peer_ids[:, None], peer_ids[None, :], 0), axis=1
    )
    run_ends = jnp.cumsum(arriving_lengths)
    starts = run_ends - arriving_lengths
    packed_ids = jnp.arange(CAP)
    source_of = jnp.sum((run_ends[None, :] <= packed_ids[:, None]).astype(jnp.int32), axis=1)
    source_hot = (source_of[:, None] == peer_ids[None, :]).astype(jnp.int32)
    token_index = packed_ids - jnp.sum(source_hot * starts[None, :], axis=1)
    positions = jnp.sum(source_hot * arriving_attach[None, :], axis=1) + token_index
    flat_index = source_of * slot_length + token_index
    slot_source = jnp.clip(starts[:, None] + slot_steps[None, :], 0, CAP - 1).reshape(-1)
    live_mask = slot_steps[None, :] < arriving_lengths[:, None]

    slot_pick = (
        (jnp.arange(CAP)[None, :] == slot_source[:, None]) & live_mask.reshape(-1)[:, None]
    ).astype(jnp.bfloat16)
    pack_pick = (
        jnp.arange(peers * slot_length)[None, :] == flat_index[:, None]
    ).astype(jnp.bfloat16)

    def to_slots(values):
        moved = jnp.dot(slot_pick, values, preferred_element_type=jnp.float32)
        return moved.astype(values.dtype).reshape((peers, slot_length) + values.shape[1:])

    def to_packed(values):
        return jnp.dot(pack_pick, values, preferred_element_type=jnp.float32).astype(values.dtype)

    tail_rows = fetch_prefix(arriving_attach, prefix_cache, block_of_slot, WINDOW)
    my_features = lax.dynamic_slice_in_dim(
        suffix_tokens, tensor_index * feature_share, feature_share, 2
    )
    send_pick = (send_order[:, None] == peer_ids[None, :]).astype(jnp.bfloat16)
    outgoing = jnp.einsum(
        "dk,ktf->dtf", send_pick, my_features, preferred_element_type=jnp.float32
    ).astype(jnp.bfloat16)
    landed = lax.all_to_all(outgoing, "req", split_axis=0, concat_axis=0, tiled=True)
    input_part = to_packed(landed.reshape(peers * slot_length, feature_share))
    input_rows = lax.all_gather(input_part, "tp", axis=1, tiled=True)
    row_total = input_part.shape[0]
    normed_in = norm_rows(input_rows, attn_gain)
    queries = jnp.dot(normed_in, w_query, preferred_element_type=jnp.float32).reshape(
        row_total, -1, head_dim
    )
    queries = rotate(queries, positions).astype(jnp.bfloat16)
    paired = jnp.dot(
        normed_in, w_keyval.reshape(features, -1), preferred_element_type=jnp.float32
    ).reshape(row_total, value_heads, 2 * head_dim)
    rotated = rotate(paired[..., :head_dim], positions)
    paired = jnp.concatenate([rotated, paired[..., head_dim:]], axis=-1).astype(jnp.bfloat16)
    attended = attend_pallas(
        to_slots(queries.reshape(row_total, -1)),
        to_slots(paired.reshape(row_total, -1)),
        tail_rows,
        sink_logits,
    ).reshape(peers * slot_length, -1)
    attended = to_packed(attended)
    partial_value = jnp.dot(attended, w_out, preferred_element_type=jnp.float32)
    summed = lax.psum_scatter(
        partial_value.astype(jnp.bfloat16), "tp", scatter_dimension=1, tiled=True
    ).astype(jnp.float32)
    residual_part = (input_part.astype(jnp.float32) + summed).astype(jnp.bfloat16)
    residual = lax.all_gather(residual_part, "tp", axis=1, tiled=True)
    normed_mid = norm_rows(residual, mlp_gain)
    gate_proj = jnp.dot(normed_mid, w_gate, preferred_element_type=jnp.float32)
    up_proj = jnp.dot(normed_mid, w_up, preferred_element_type=jnp.float32)
    hidden = (jax.nn.silu(gate_proj) * up_proj).astype(jnp.bfloat16)
    down_sum = lax.psum_scatter(
        jnp.dot(hidden, w_down, preferred_element_type=jnp.float32).astype(jnp.bfloat16),
        "tp",
        scatter_dimension=1,
        tiled=True,
    ).astype(jnp.float32)
    out_rows = (residual_part.astype(jnp.float32) + down_sum).astype(jnp.bfloat16)
    out_slots = to_slots(out_rows)
    returned = lax.all_to_all(out_slots, "req", split_axis=0, concat_axis=0, tiled=True)
    return_pick = (my_row[:, None] == peer_ids[None, :]).astype(jnp.bfloat16)
    return jnp.einsum(
        "kd,dtf->ktf", return_pick, returned, preferred_element_type=jnp.float32
    ).astype(jnp.bfloat16)


def solution(mesh):
    in_specs = (
        P("req", None, None),
        P(),
        P(),
        P(),
        P("req", None, "tp", None),
        P(),
        P("tp"),
        P(),
        P(None, "tp"),
        P(None, "tp", None),
        P("tp", None),
        P(),
        P(None, "tp"),
        P(None, "tp"),
        P("tp", None),
    )
    out_specs = P("req", None, "tp")
    return jax.shard_map(local, mesh=mesh, in_specs=in_specs, out_specs=out_specs, check_vma=False)
```

```python
import jax
import jax.numpy as jnp
from jax import lax
from jax.sharding import PartitionSpec as P
from jax.experimental import pallas as pl
from jax.experimental.pallas import tpu as pltpu

WINDOW = 128
CAP = 768


ROPE_BASE = 150000.0
EPSILON = 1e-05


def norm_rows(inputs, gains):
    widened = inputs.astype(jnp.float32)
    factor = lax.rsqrt(jnp.mean(widened * widened, axis=-1, keepdims=True) + EPSILON)
    return (widened * factor * gains.astype(jnp.float32)).astype(jnp.bfloat16)


def rotate(vectors, positions):
    half_dim = vectors.shape[-1] // 2
    frequency = ROPE_BASE ** (-(jnp.arange(half_dim).astype(jnp.float32) * 2.0 / vectors.shape[-1]))
    angles = positions.astype(jnp.float32)[:, None, None] * frequency
    cosine = jnp.cos(angles)
    sine_part = jnp.sin(angles)
    first_half = vectors[..., :half_dim]
    second = vectors[..., half_dim:]
    return jnp.concatenate(
        [first_half * cosine - second * sine_part, second * cosine + first_half * sine_part],
        axis=-1,
    )


def attend(query_slots, paired_slots, tail_rows, sink_logits):
    peers, slot_length = (query_slots.shape[0], query_slots.shape[1])
    value_heads = paired_slots.shape[2]
    head_dim = paired_slots.shape[3] // 2
    group_size = query_slots.shape[2] // value_heads
    window = tail_rows.shape[1]
    grouped_query = query_slots.reshape(peers, slot_length, value_heads, group_size, head_dim)
    near_keys = jnp.concatenate([tail_rows, paired_slots], axis=1)
    score_scale = head_dim ** (-0.5)
    near_scores = (
        jnp.einsum(
            "ntkgd,nskd->nkgts",
            grouped_query,
            near_keys[..., :head_dim],
            preferred_element_type=jnp.float32,
        )
        * score_scale
    )
    sink_scores = sink_logits.reshape(value_heads, group_size)[None, :, :, None, None]
    slot_steps = jnp.arange(slot_length)
    columns = jnp.arange(window + slot_length)
    allowed = jnp.where(
        columns[None, :] < window,
        columns[None, :] > slot_steps[:, None],
        columns[None, :] - window <= slot_steps[:, None],
    )
    near_scores = jnp.where(allowed, near_scores, -jnp.inf)
    largest = jnp.maximum(jnp.max(near_scores, axis=-1, keepdims=True), sink_scores)
    near_weights = jnp.exp(near_scores - largest)
    normalizer = jnp.sum(near_weights, axis=-1, keepdims=True) + jnp.exp(sink_scores - largest)
    near_weights = (near_weights / normalizer).astype(jnp.bfloat16)
    mixed = jnp.einsum(
        "nkgts,nskd->ntkgd",
        near_weights,
        near_keys[..., head_dim:],
        preferred_element_type=jnp.float32,
    )
    return mixed.astype(jnp.bfloat16).reshape(
        peers * slot_length, value_heads * group_size * head_dim
    )


def attend_kernel(sink_ref, q_ref, kv_ref, tail_ref, o_ref):
    batch, slot_length = q_ref.shape[0], q_ref.shape[1]
    window = tail_ref.shape[1]
    head_dim = kv_ref.shape[2] // 2
    heads = q_ref.shape[2] // head_dim
    scale = head_dim ** (-0.5)
    step = lax.broadcasted_iota(jnp.int32, (slot_length, window), 0)
    column = lax.broadcasted_iota(jnp.int32, (slot_length, window), 1)
    tail_allowed = jnp.concatenate([column > step] * heads, axis=0)
    own_step = lax.broadcasted_iota(jnp.int32, (slot_length, slot_length), 0)
    own_column = lax.broadcasted_iota(jnp.int32, (slot_length, slot_length), 1)
    own_allowed = jnp.concatenate([own_column <= own_step] * heads, axis=0)
    sink = jnp.concatenate(
        [jnp.full((slot_length, 1), sink_ref[head], jnp.float32) for head in range(heads)],
        axis=0,
    )
    contract = (((1,), (1,)), ((), ()))
    for item in range(batch):
        kv = kv_ref[item]
        tail = tail_ref[item]
        query = q_ref[item]
        stacked = jnp.concatenate(
            [query[:, head * head_dim:(head + 1) * head_dim] for head in range(heads)], axis=0
        )
        tail_scores = lax.dot_general(
            stacked, tail[:, :head_dim], contract, preferred_element_type=jnp.float32
        ) * scale
        own_scores = lax.dot_general(
            stacked, kv[:, :head_dim], contract, preferred_element_type=jnp.float32
        ) * scale
        tail_scores = jnp.where(tail_allowed, tail_scores, -jnp.inf)
        own_scores = jnp.where(own_allowed, own_scores, -jnp.inf)
        largest = jnp.maximum(
            jnp.maximum(
                jnp.max(tail_scores, axis=1, keepdims=True),
                jnp.max(own_scores, axis=1, keepdims=True),
            ),
            sink,
        )
        tail_weights = jnp.exp(tail_scores - largest)
        own_weights = jnp.exp(own_scores - largest)
        normalizer = (
            jnp.sum(tail_weights, axis=1, keepdims=True)
            + jnp.sum(own_weights, axis=1, keepdims=True)
            + jnp.exp(sink - largest)
        )
        inverse = 1.0 / normalizer
        tail_weights = (tail_weights * inverse).astype(jnp.bfloat16)
        own_weights = (own_weights * inverse).astype(jnp.bfloat16)
        mixed = jnp.dot(
            tail_weights, tail[:, head_dim:], preferred_element_type=jnp.float32
        ) + jnp.dot(own_weights, kv[:, head_dim:], preferred_element_type=jnp.float32)
        mixed = mixed.astype(o_ref.dtype)
        for head in range(heads):
            o_ref[item, :, head * head_dim:(head + 1) * head_dim] = mixed[
                head * slot_length:(head + 1) * slot_length
            ]


def attend_pallas(query_slots, paired_slots, tail_rows, sink_logits, batch=2):
    peers, slot_length, width = query_slots.shape
    window = tail_rows.shape[1]
    pair_width = paired_slots.shape[2]
    head_dim = pair_width // 2
    heads = width // head_dim
    flops = peers * heads * 4 * slot_length * (window + slot_length) * head_dim
    moved = 2 * (2 * query_slots.size + paired_slots.size + tail_rows.size)
    return pl.pallas_call(
        attend_kernel,
        grid=(peers // batch,),
        in_specs=[
            pl.BlockSpec(memory_space=pltpu.SMEM),
            pl.BlockSpec((batch, slot_length, width), lambda n: (n, 0, 0)),
            pl.BlockSpec((batch, slot_length, pair_width), lambda n: (n, 0, 0)),
            pl.BlockSpec((batch, window, pair_width), lambda n: (n, 0, 0)),
        ],
        out_specs=pl.BlockSpec((batch, slot_length, width), lambda n: (n, 0, 0)),
        out_shape=jax.ShapeDtypeStruct((peers, slot_length, width), jnp.bfloat16),
        cost_estimate=pl.CostEstimate(
            flops=flops,
            transcendentals=peers * heads * slot_length * (window + slot_length),
            bytes_accessed=moved,
        ),
    )(sink_logits.astype(jnp.float32), query_slots, paired_slots, tail_rows)


def fetch_prefix(attach_slots, prefix_cache, block_of_slot, window):
    total_blocks = block_of_slot.shape[0]
    block_len = prefix_cache.shape[1]
    catalog = jnp.arange(total_blocks)
    home_row = jnp.sum(
        jnp.where(block_of_slot[None, :] == catalog[:, None], catalog[None, :], 0), axis=1
    )
    first_block = jnp.clip((attach_slots - window) // block_len, 0, total_blocks - 1)
    second_block = jnp.clip(first_block + 1, 0, total_blocks - 1)
    offset = attach_slots - window - first_block * block_len
    shard_rows = lax.all_gather(prefix_cache, "req", axis=0, tiled=True)
    shard_rows = shard_rows.reshape(total_blocks, block_len, -1)
    pair = jnp.stack([home_row[first_block], home_row[second_block]], axis=1)
    both = shard_rows[pair].reshape(attach_slots.shape[0], 2 * block_len, -1)
    picks = (
        jnp.arange(2 * block_len)[None, None, :]
        == offset[:, None, None] + jnp.arange(window)[None, :, None]
    ).astype(jnp.bfloat16)
    return jnp.einsum(
        "ruk,rkd->rud", picks, both, preferred_element_type=jnp.float32
    ).astype(jnp.bfloat16)


def local(
    suffix_tokens,
    route_lengths,
    dest_perm,
    attach_points,
    prefix_cache,
    block_of_slot,
    sink_logits,
    attn_gain,
    w_query,
    w_keyval,
    w_out,
    mlp_gain,
    w_gate,
    w_up,
    w_down,
):
    peers = lax.axis_size("req")
    splits = lax.axis_size("tp")
    request_index = lax.axis_index("req")
    tensor_index = lax.axis_index("tp")
    slot_count, slot_length, features = suffix_tokens.shape
    feature_share = features // splits
    value_heads = w_keyval.shape[1]
    head_dim = w_keyval.shape[2] // 2
    peer_ids = jnp.arange(peers)
    slot_steps = jnp.arange(slot_length)
    my_row = lax.dynamic_index_in_dim(dest_perm, request_index, 0, keepdims=False)
    attach_table = attach_points.reshape(peers, peers)
    arriving_lengths = lax.dynamic_index_in_dim(route_lengths, request_index, 0, keepdims=False)
    arriving = (dest_perm == request_index).astype(jnp.int32)
    arriving_attach = jnp.sum(attach_table * arriving, axis=1)
    send_order = jnp.sum(
        jnp.where(my_row[None, :] == peer_ids[:, None], peer_ids[None, :], 0), axis=1
    )
    run_ends = jnp.cumsum(arriving_lengths)
    starts = run_ends - arriving_lengths
    packed_ids = jnp.arange(CAP)
    source_of = jnp.sum((run_ends[None, :] <= packed_ids[:, None]).astype(jnp.int32), axis=1)
    source_hot = (source_of[:, None] == peer_ids[None, :]).astype(jnp.int32)
    token_index = packed_ids - jnp.sum(source_hot * starts[None, :], axis=1)
    positions = jnp.sum(source_hot * arriving_attach[None, :], axis=1) + token_index
    flat_index = source_of * slot_length + token_index
    slot_source = jnp.clip(starts[:, None] + slot_steps[None, :], 0, CAP - 1).reshape(-1)
    live_mask = slot_steps[None, :] < arriving_lengths[:, None]

    slot_pick = (
        (jnp.arange(CAP)[None, :] == slot_source[:, None]) & live_mask.reshape(-1)[:, None]
    ).astype(jnp.bfloat16)
    pack_pick = (
        jnp.arange(peers * slot_length)[None, :] == flat_index[:, None]
    ).astype(jnp.bfloat16)

    def to_slots(values):
        moved = jnp.dot(slot_pick, values, preferred_element_type=jnp.float32)
        return moved.astype(values.dtype).reshape((peers, slot_length) + values.shape[1:])

    def to_packed(values):
        return jnp.dot(pack_pick, values, preferred_element_type=jnp.float32).astype(values.dtype)

    my_features = lax.dynamic_slice_in_dim(
        suffix_tokens, tensor_index * feature_share, feature_share, 2
    )
    send_pick = (send_order[:, None] == peer_ids[None, :]).astype(jnp.bfloat16)
    outgoing = jnp.einsum(
        "dk,ktf->dtf", send_pick, my_features, preferred_element_type=jnp.float32
    ).astype(jnp.bfloat16)
    landed = lax.all_to_all(outgoing, "req", split_axis=0, concat_axis=0, tiled=True)
    input_part = to_packed(landed.reshape(peers * slot_length, feature_share))
    input_rows = lax.all_gather(input_part, "tp", axis=1, tiled=True)
    row_total = input_part.shape[0]
    prefix_after, input_rows = lax.optimization_barrier((prefix_cache, input_rows))
    tail_rows = fetch_prefix(arriving_attach, prefix_after, block_of_slot, WINDOW)
    normed_in = norm_rows(input_rows, attn_gain)
    queries = jnp.dot(normed_in, w_query, preferred_element_type=jnp.float32).reshape(
        row_total, -1, head_dim
    )
    queries = rotate(queries, positions).astype(jnp.bfloat16)
    paired = jnp.dot(
        normed_in, w_keyval.reshape(features, -1), preferred_element_type=jnp.float32
    ).reshape(row_total, value_heads, 2 * head_dim)
    rotated = rotate(paired[..., :head_dim], positions)
    paired = jnp.concatenate([rotated, paired[..., head_dim:]], axis=-1).astype(jnp.bfloat16)
    attended = attend_pallas(
        to_slots(queries.reshape(row_total, -1)),
        to_slots(paired.reshape(row_total, -1)),
        tail_rows,
        sink_logits,
    ).reshape(peers * slot_length, -1)
    attended = to_packed(attended)
    partial_value = jnp.dot(attended, w_out, preferred_element_type=jnp.float32)
    summed = lax.psum_scatter(
        partial_value.astype(jnp.bfloat16), "tp", scatter_dimension=1, tiled=True
    ).astype(jnp.float32)
    residual_part = (input_part.astype(jnp.float32) + summed).astype(jnp.bfloat16)
    residual = lax.all_gather(residual_part, "tp", axis=1, tiled=True)
    normed_mid = norm_rows(residual, mlp_gain)
    gate_proj = jnp.dot(normed_mid, w_gate, preferred_element_type=jnp.float32)
    up_proj = jnp.dot(normed_mid, w_up, preferred_element_type=jnp.float32)
    hidden = (jax.nn.silu(gate_proj) * up_proj).astype(jnp.bfloat16)
    down_sum = lax.psum_scatter(
        jnp.dot(hidden, w_down, preferred_element_type=jnp.float32).astype(jnp.bfloat16),
        "tp",
        scatter_dimension=1,
        tiled=True,
    ).astype(jnp.float32)
    out_rows = (residual_part.astype(jnp.float32) + down_sum).astype(jnp.bfloat16)
    out_slots = to_slots(out_rows)
    returned = lax.all_to_all(out_slots, "req", split_axis=0, concat_axis=0, tiled=True)
    return_pick = (my_row[:, None] == peer_ids[None, :]).astype(jnp.bfloat16)
    return jnp.einsum(
        "kd,dtf->ktf", return_pick, returned, preferred_element_type=jnp.float32
    ).astype(jnp.bfloat16)


def solution(mesh):
    in_specs = (
        P("req", None, None),
        P(),
        P(),
        P(),
        P("req", None, "tp", None),
        P(),
        P("tp"),
        P(),
        P(None, "tp"),
        P(None, "tp", None),
        P("tp", None),
        P(),
        P(None, "tp"),
        P(None, "tp"),
        P("tp", None),
    )
    out_specs = P("req", None, "tp")
    return jax.shard_map(local, mesh=mesh, in_specs=in_specs, out_specs=out_specs, check_vma=False)
```

```python
import jax
import jax.numpy as jnp
from jax import lax
from jax.sharding import PartitionSpec as P
from jax.experimental import pallas as pl
from jax.experimental.pallas import tpu as pltpu

WINDOW = 128
CAP = 768


ROPE_BASE = 150000.0
EPSILON = 1e-05


def norm_rows(inputs, gains):
    widened = inputs.astype(jnp.float32)
    factor = lax.rsqrt(jnp.mean(widened * widened, axis=-1, keepdims=True) + EPSILON)
    return (widened * factor * gains.astype(jnp.float32)).astype(jnp.bfloat16)


def rotate(vectors, positions):
    half_dim = vectors.shape[-1] // 2
    frequency = ROPE_BASE ** (-(jnp.arange(half_dim).astype(jnp.float32) * 2.0 / vectors.shape[-1]))
    angles = positions.astype(jnp.float32)[:, None, None] * frequency
    cosine = jnp.cos(angles)
    sine_part = jnp.sin(angles)
    first_half = vectors[..., :half_dim]
    second = vectors[..., half_dim:]
    return jnp.concatenate(
        [first_half * cosine - second * sine_part, second * cosine + first_half * sine_part],
        axis=-1,
    )


def attend(query_slots, paired_slots, tail_rows, sink_logits):
    peers, slot_length = (query_slots.shape[0], query_slots.shape[1])
    value_heads = paired_slots.shape[2]
    head_dim = paired_slots.shape[3] // 2
    group_size = query_slots.shape[2] // value_heads
    window = tail_rows.shape[1]
    grouped_query = query_slots.reshape(peers, slot_length, value_heads, group_size, head_dim)
    near_keys = jnp.concatenate([tail_rows, paired_slots], axis=1)
    score_scale = head_dim ** (-0.5)
    near_scores = (
        jnp.einsum(
            "ntkgd,nskd->nkgts",
            grouped_query,
            near_keys[..., :head_dim],
            preferred_element_type=jnp.float32,
        )
        * score_scale
    )
    sink_scores = sink_logits.reshape(value_heads, group_size)[None, :, :, None, None]
    slot_steps = jnp.arange(slot_length)
    columns = jnp.arange(window + slot_length)
    allowed = jnp.where(
        columns[None, :] < window,
        columns[None, :] > slot_steps[:, None],
        columns[None, :] - window <= slot_steps[:, None],
    )
    near_scores = jnp.where(allowed, near_scores, -jnp.inf)
    largest = jnp.maximum(jnp.max(near_scores, axis=-1, keepdims=True), sink_scores)
    near_weights = jnp.exp(near_scores - largest)
    normalizer = jnp.sum(near_weights, axis=-1, keepdims=True) + jnp.exp(sink_scores - largest)
    near_weights = (near_weights / normalizer).astype(jnp.bfloat16)
    mixed = jnp.einsum(
        "nkgts,nskd->ntkgd",
        near_weights,
        near_keys[..., head_dim:],
        preferred_element_type=jnp.float32,
    )
    return mixed.astype(jnp.bfloat16).reshape(
        peers * slot_length, value_heads * group_size * head_dim
    )


def attend_kernel(sink_ref, q_ref, kv_ref, tail_ref, o_ref):
    batch, slot_length = q_ref.shape[0], q_ref.shape[1]
    window = tail_ref.shape[1]
    head_dim = kv_ref.shape[2] // 2
    heads = q_ref.shape[2] // head_dim
    scale = head_dim ** (-0.5)
    step = lax.broadcasted_iota(jnp.int32, (slot_length, window), 0)
    column = lax.broadcasted_iota(jnp.int32, (slot_length, window), 1)
    tail_allowed = jnp.concatenate([column > step] * heads, axis=0)
    own_step = lax.broadcasted_iota(jnp.int32, (slot_length, slot_length), 0)
    own_column = lax.broadcasted_iota(jnp.int32, (slot_length, slot_length), 1)
    own_allowed = jnp.concatenate([own_column <= own_step] * heads, axis=0)
    sink = jnp.concatenate(
        [jnp.full((slot_length, 1), sink_ref[head], jnp.float32) for head in range(heads)],
        axis=0,
    )
    contract = (((1,), (1,)), ((), ()))
    for item in range(batch):
        kv = kv_ref[item]
        tail = tail_ref[item]
        query = q_ref[item]
        stacked = jnp.concatenate(
            [query[:, head * head_dim:(head + 1) * head_dim] for head in range(heads)], axis=0
        )
        tail_scores = lax.dot_general(
            stacked, tail[:, :head_dim], contract, preferred_element_type=jnp.float32
        ) * scale
        own_scores = lax.dot_general(
            stacked, kv[:, :head_dim], contract, preferred_element_type=jnp.float32
        ) * scale
        tail_scores = jnp.where(tail_allowed, tail_scores, -jnp.inf)
        own_scores = jnp.where(own_allowed, own_scores, -jnp.inf)
        largest = jnp.maximum(
            jnp.maximum(
                jnp.max(tail_scores, axis=1, keepdims=True),
                jnp.max(own_scores, axis=1, keepdims=True),
            ),
            sink,
        )
        tail_weights = jnp.exp(tail_scores - largest)
        own_weights = jnp.exp(own_scores - largest)
        normalizer = (
            jnp.sum(tail_weights, axis=1, keepdims=True)
            + jnp.sum(own_weights, axis=1, keepdims=True)
            + jnp.exp(sink - largest)
        )
        inverse = 1.0 / normalizer
        tail_weights = (tail_weights * inverse).astype(jnp.bfloat16)
        own_weights = (own_weights * inverse).astype(jnp.bfloat16)
        mixed = jnp.dot(
            tail_weights, tail[:, head_dim:], preferred_element_type=jnp.float32
        ) + jnp.dot(own_weights, kv[:, head_dim:], preferred_element_type=jnp.float32)
        mixed = mixed.astype(o_ref.dtype)
        for head in range(heads):
            o_ref[item, :, head * head_dim:(head + 1) * head_dim] = mixed[
                head * slot_length:(head + 1) * slot_length
            ]


def attend_pallas(query_slots, paired_slots, tail_rows, sink_logits, batch=2):
    peers, slot_length, width = query_slots.shape
    window = tail_rows.shape[1]
    pair_width = paired_slots.shape[2]
    head_dim = pair_width // 2
    heads = width // head_dim
    flops = peers * heads * 4 * slot_length * (window + slot_length) * head_dim
    moved = 2 * (2 * query_slots.size + paired_slots.size + tail_rows.size)
    return pl.pallas_call(
        attend_kernel,
        grid=(peers // batch,),
        in_specs=[
            pl.BlockSpec(memory_space=pltpu.SMEM),
            pl.BlockSpec((batch, slot_length, width), lambda n: (n, 0, 0)),
            pl.BlockSpec((batch, slot_length, pair_width), lambda n: (n, 0, 0)),
            pl.BlockSpec((batch, window, pair_width), lambda n: (n, 0, 0)),
        ],
        out_specs=pl.BlockSpec((batch, slot_length, width), lambda n: (n, 0, 0)),
        out_shape=jax.ShapeDtypeStruct((peers, slot_length, width), jnp.bfloat16),
        cost_estimate=pl.CostEstimate(
            flops=flops,
            transcendentals=peers * heads * slot_length * (window + slot_length),
            bytes_accessed=moved,
        ),
    )(sink_logits.astype(jnp.float32), query_slots, paired_slots, tail_rows)


def fetch_prefix(attach_slots, early_rows, late_half, half, block_of_slot, window):
    total_blocks = block_of_slot.shape[0]
    block_len = early_rows.shape[1]
    peers = lax.axis_size("req")
    catalog = jnp.arange(total_blocks)
    home_row = jnp.sum(
        jnp.where(block_of_slot[None, :] == catalog[:, None], catalog[None, :], 0), axis=1
    )
    first_block = jnp.clip((attach_slots - window) // block_len, 0, total_blocks - 1)
    second_block = jnp.clip(first_block + 1, 0, total_blocks - 1)
    offset = attach_slots - window - first_block * block_len
    late_rows = lax.all_gather(late_half, "req", axis=0, tiled=True)
    shard_rows = jnp.concatenate([early_rows, late_rows], axis=0)
    shard_rows = shard_rows.reshape(total_blocks, block_len, -1)
    stored = jnp.stack([home_row[first_block], home_row[second_block]], axis=1)
    owner, local_slot = stored // (2 * half), stored % (2 * half)
    pair = (local_slot // half) * (peers * half) + owner * half + local_slot % half
    both = shard_rows[pair].reshape(attach_slots.shape[0], 2 * block_len, -1)
    picks = (
        jnp.arange(2 * block_len)[None, None, :]
        == offset[:, None, None] + jnp.arange(window)[None, :, None]
    ).astype(jnp.bfloat16)
    return jnp.einsum(
        "ruk,rkd->rud", picks, both, preferred_element_type=jnp.float32
    ).astype(jnp.bfloat16)


def local(
    suffix_tokens,
    route_lengths,
    dest_perm,
    attach_points,
    prefix_cache,
    block_of_slot,
    sink_logits,
    attn_gain,
    w_query,
    w_keyval,
    w_out,
    mlp_gain,
    w_gate,
    w_up,
    w_down,
):
    peers = lax.axis_size("req")
    splits = lax.axis_size("tp")
    request_index = lax.axis_index("req")
    tensor_index = lax.axis_index("tp")
    slot_count, slot_length, features = suffix_tokens.shape
    feature_share = features // splits
    value_heads = w_keyval.shape[1]
    head_dim = w_keyval.shape[2] // 2
    peer_ids = jnp.arange(peers)
    slot_steps = jnp.arange(slot_length)
    my_row = lax.dynamic_index_in_dim(dest_perm, request_index, 0, keepdims=False)
    attach_table = attach_points.reshape(peers, peers)
    arriving_lengths = lax.dynamic_index_in_dim(route_lengths, request_index, 0, keepdims=False)
    arriving = (dest_perm == request_index).astype(jnp.int32)
    arriving_attach = jnp.sum(attach_table * arriving, axis=1)
    send_order = jnp.sum(
        jnp.where(my_row[None, :] == peer_ids[:, None], peer_ids[None, :], 0), axis=1
    )
    run_ends = jnp.cumsum(arriving_lengths)
    starts = run_ends - arriving_lengths
    packed_ids = jnp.arange(CAP)
    source_of = jnp.sum((run_ends[None, :] <= packed_ids[:, None]).astype(jnp.int32), axis=1)
    source_hot = (source_of[:, None] == peer_ids[None, :]).astype(jnp.int32)
    token_index = packed_ids - jnp.sum(source_hot * starts[None, :], axis=1)
    positions = jnp.sum(source_hot * arriving_attach[None, :], axis=1) + token_index
    flat_index = source_of * slot_length + token_index
    slot_source = jnp.clip(starts[:, None] + slot_steps[None, :], 0, CAP - 1).reshape(-1)
    live_mask = slot_steps[None, :] < arriving_lengths[:, None]

    slot_pick = (
        (jnp.arange(CAP)[None, :] == slot_source[:, None]) & live_mask.reshape(-1)[:, None]
    ).astype(jnp.bfloat16)
    pack_pick = (
        jnp.arange(peers * slot_length)[None, :] == flat_index[:, None]
    ).astype(jnp.bfloat16)

    def to_slots(values):
        moved = jnp.dot(slot_pick, values, preferred_element_type=jnp.float32)
        return moved.astype(values.dtype).reshape((peers, slot_length) + values.shape[1:])

    def to_packed(values):
        return jnp.dot(pack_pick, values, preferred_element_type=jnp.float32).astype(values.dtype)

    my_features = lax.dynamic_slice_in_dim(
        suffix_tokens, tensor_index * feature_share, feature_share, 2
    )
    send_pick = (send_order[:, None] == peer_ids[None, :]).astype(jnp.bfloat16)
    outgoing = jnp.einsum(
        "dk,ktf->dtf", send_pick, my_features, preferred_element_type=jnp.float32
    ).astype(jnp.bfloat16)
    landed = lax.all_to_all(outgoing, "req", split_axis=0, concat_axis=0, tiled=True)
    input_part = to_packed(landed.reshape(peers * slot_length, feature_share))
    held_here = prefix_cache.shape[0]
    early_rows = lax.all_gather(prefix_cache[:held_here // 2], "req", axis=0, tiled=True)
    input_part, early_rows = lax.optimization_barrier((input_part, early_rows))
    input_rows = lax.all_gather(input_part, "tp", axis=1, tiled=True)
    row_total = input_part.shape[0]
    late_half, input_rows = lax.optimization_barrier(
        (prefix_cache[held_here // 2:], input_rows)
    )
    tail_rows = fetch_prefix(
        arriving_attach, early_rows, late_half, held_here // 2, block_of_slot, WINDOW
    )
    normed_in = norm_rows(input_rows, attn_gain)
    queries = jnp.dot(normed_in, w_query, preferred_element_type=jnp.float32).reshape(
        row_total, -1, head_dim
    )
    queries = rotate(queries, positions).astype(jnp.bfloat16)
    paired = jnp.dot(
        normed_in, w_keyval.reshape(features, -1), preferred_element_type=jnp.float32
    ).reshape(row_total, value_heads, 2 * head_dim)
    rotated = rotate(paired[..., :head_dim], positions)
    paired = jnp.concatenate([rotated, paired[..., head_dim:]], axis=-1).astype(jnp.bfloat16)
    attended = attend_pallas(
        to_slots(queries.reshape(row_total, -1)),
        to_slots(paired.reshape(row_total, -1)),
        tail_rows,
        sink_logits,
    ).reshape(peers * slot_length, -1)
    attended = to_packed(attended)
    partial_value = jnp.dot(attended, w_out, preferred_element_type=jnp.float32)
    summed = lax.psum_scatter(
        partial_value.astype(jnp.bfloat16), "tp", scatter_dimension=1, tiled=True
    ).astype(jnp.float32)
    residual_part = (input_part.astype(jnp.float32) + summed).astype(jnp.bfloat16)
    residual = lax.all_gather(residual_part, "tp", axis=1, tiled=True)
    normed_mid = norm_rows(residual, mlp_gain)
    gate_proj = jnp.dot(normed_mid, w_gate, preferred_element_type=jnp.float32)
    up_proj = jnp.dot(normed_mid, w_up, preferred_element_type=jnp.float32)
    hidden = (jax.nn.silu(gate_proj) * up_proj).astype(jnp.bfloat16)
    down_sum = lax.psum_scatter(
        jnp.dot(hidden, w_down, preferred_element_type=jnp.float32).astype(jnp.bfloat16),
        "tp",
        scatter_dimension=1,
        tiled=True,
    ).astype(jnp.float32)
    out_rows = (residual_part.astype(jnp.float32) + down_sum).astype(jnp.bfloat16)
    out_slots = to_slots(out_rows)
    returned = lax.all_to_all(out_slots, "req", split_axis=0, concat_axis=0, tiled=True)
    return_pick = (my_row[:, None] == peer_ids[None, :]).astype(jnp.bfloat16)
    return jnp.einsum(
        "kd,dtf->ktf", return_pick, returned, preferred_element_type=jnp.float32
    ).astype(jnp.bfloat16)


def solution(mesh):
    in_specs = (
        P("req", None, None),
        P(),
        P(),
        P(),
        P("req", None, "tp", None),
        P(),
        P("tp"),
        P(),
        P(None, "tp"),
        P(None, "tp", None),
        P("tp", None),
        P(),
        P(None, "tp"),
        P(None, "tp"),
        P("tp", None),
    )
    out_specs = P("req", None, "tp")
    return jax.shard_map(local, mesh=mesh, in_specs=in_specs, out_specs=out_specs, check_vma=False)
```

```python
import jax
import jax.numpy as jnp
from jax import lax
from jax.sharding import PartitionSpec as P
from jax.experimental import pallas as pl
from jax.experimental.pallas import tpu as pltpu

WINDOW = 128
CAP = 768


ROPE_BASE = 150000.0
EPSILON = 1e-05


def norm_rows(inputs, gains):
    widened = inputs.astype(jnp.float32)
    factor = lax.rsqrt(jnp.mean(widened * widened, axis=-1, keepdims=True) + EPSILON)
    return (widened * factor * gains.astype(jnp.float32)).astype(jnp.bfloat16)


def rotate(vectors, positions):
    half_dim = vectors.shape[-1] // 2
    frequency = ROPE_BASE ** (-(jnp.arange(half_dim).astype(jnp.float32) * 2.0 / vectors.shape[-1]))
    angles = positions.astype(jnp.float32)[:, None, None] * frequency
    cosine = jnp.cos(angles)
    sine_part = jnp.sin(angles)
    first_half = vectors[..., :half_dim]
    second = vectors[..., half_dim:]
    return jnp.concatenate(
        [first_half * cosine - second * sine_part, second * cosine + first_half * sine_part],
        axis=-1,
    )


def attend(query_slots, paired_slots, tail_rows, sink_logits):
    peers, slot_length = (query_slots.shape[0], query_slots.shape[1])
    value_heads = paired_slots.shape[2]
    head_dim = paired_slots.shape[3] // 2
    group_size = query_slots.shape[2] // value_heads
    window = tail_rows.shape[1]
    grouped_query = query_slots.reshape(peers, slot_length, value_heads, group_size, head_dim)
    near_keys = jnp.concatenate([tail_rows, paired_slots], axis=1)
    score_scale = head_dim ** (-0.5)
    near_scores = (
        jnp.einsum(
            "ntkgd,nskd->nkgts",
            grouped_query,
            near_keys[..., :head_dim],
            preferred_element_type=jnp.float32,
        )
        * score_scale
    )
    sink_scores = sink_logits.reshape(value_heads, group_size)[None, :, :, None, None]
    slot_steps = jnp.arange(slot_length)
    columns = jnp.arange(window + slot_length)
    allowed = jnp.where(
        columns[None, :] < window,
        columns[None, :] > slot_steps[:, None],
        columns[None, :] - window <= slot_steps[:, None],
    )
    near_scores = jnp.where(allowed, near_scores, -jnp.inf)
    largest = jnp.maximum(jnp.max(near_scores, axis=-1, keepdims=True), sink_scores)
    near_weights = jnp.exp(near_scores - largest)
    normalizer = jnp.sum(near_weights, axis=-1, keepdims=True) + jnp.exp(sink_scores - largest)
    near_weights = (near_weights / normalizer).astype(jnp.bfloat16)
    mixed = jnp.einsum(
        "nkgts,nskd->ntkgd",
        near_weights,
        near_keys[..., head_dim:],
        preferred_element_type=jnp.float32,
    )
    return mixed.astype(jnp.bfloat16).reshape(
        peers * slot_length, value_heads * group_size * head_dim
    )


def attend_kernel(sink_ref, q_ref, kv_ref, tail_ref, o_ref):
    batch, slot_length = q_ref.shape[0], q_ref.shape[1]
    window = tail_ref.shape[1]
    head_dim = kv_ref.shape[2] // 2
    heads = q_ref.shape[2] // head_dim
    scale = head_dim ** (-0.5)
    step = lax.broadcasted_iota(jnp.int32, (slot_length, window), 0)
    column = lax.broadcasted_iota(jnp.int32, (slot_length, window), 1)
    tail_allowed = jnp.concatenate([column > step] * heads, axis=0)
    own_step = lax.broadcasted_iota(jnp.int32, (slot_length, slot_length), 0)
    own_column = lax.broadcasted_iota(jnp.int32, (slot_length, slot_length), 1)
    own_allowed = jnp.concatenate([own_column <= own_step] * heads, axis=0)
    sink = jnp.concatenate(
        [jnp.full((slot_length, 1), sink_ref[head], jnp.float32) for head in range(heads)],
        axis=0,
    )
    contract = (((1,), (1,)), ((), ()))
    for item in range(batch):
        kv = kv_ref[item]
        tail = tail_ref[item]
        query = q_ref[item]
        stacked = jnp.concatenate(
            [query[:, head * head_dim:(head + 1) * head_dim] for head in range(heads)], axis=0
        )
        tail_scores = lax.dot_general(
            stacked, tail[:, :head_dim], contract, preferred_element_type=jnp.float32
        ) * scale
        own_scores = lax.dot_general(
            stacked, kv[:, :head_dim], contract, preferred_element_type=jnp.float32
        ) * scale
        tail_scores = jnp.where(tail_allowed, tail_scores, -jnp.inf)
        own_scores = jnp.where(own_allowed, own_scores, -jnp.inf)
        largest = jnp.maximum(
            jnp.maximum(
                jnp.max(tail_scores, axis=1, keepdims=True),
                jnp.max(own_scores, axis=1, keepdims=True),
            ),
            sink,
        )
        tail_weights = jnp.exp(tail_scores - largest)
        own_weights = jnp.exp(own_scores - largest)
        normalizer = (
            jnp.sum(tail_weights, axis=1, keepdims=True)
            + jnp.sum(own_weights, axis=1, keepdims=True)
            + jnp.exp(sink - largest)
        )
        inverse = 1.0 / normalizer
        tail_weights = (tail_weights * inverse).astype(jnp.bfloat16)
        own_weights = (own_weights * inverse).astype(jnp.bfloat16)
        mixed = jnp.dot(
            tail_weights, tail[:, head_dim:], preferred_element_type=jnp.float32
        ) + jnp.dot(own_weights, kv[:, head_dim:], preferred_element_type=jnp.float32)
        mixed = mixed.astype(o_ref.dtype)
        for head in range(heads):
            o_ref[item, :, head * head_dim:(head + 1) * head_dim] = mixed[
                head * slot_length:(head + 1) * slot_length
            ]


def attend_pallas(query_slots, paired_slots, tail_rows, sink_logits, batch=2):
    peers, slot_length, width = query_slots.shape
    window = tail_rows.shape[1]
    pair_width = paired_slots.shape[2]
    head_dim = pair_width // 2
    heads = width // head_dim
    flops = peers * heads * 4 * slot_length * (window + slot_length) * head_dim
    moved = 2 * (2 * query_slots.size + paired_slots.size + tail_rows.size)
    return pl.pallas_call(
        attend_kernel,
        grid=(peers // batch,),
        in_specs=[
            pl.BlockSpec(memory_space=pltpu.SMEM),
            pl.BlockSpec((batch, slot_length, width), lambda n: (n, 0, 0)),
            pl.BlockSpec((batch, slot_length, pair_width), lambda n: (n, 0, 0)),
            pl.BlockSpec((batch, window, pair_width), lambda n: (n, 0, 0)),
        ],
        out_specs=pl.BlockSpec((batch, slot_length, width), lambda n: (n, 0, 0)),
        out_shape=jax.ShapeDtypeStruct((peers, slot_length, width), jnp.bfloat16),
        cost_estimate=pl.CostEstimate(
            flops=flops,
            transcendentals=peers * heads * slot_length * (window + slot_length),
            bytes_accessed=moved,
        ),
    )(sink_logits.astype(jnp.float32), query_slots, paired_slots, tail_rows)


def fetch_prefix(attach_slots, shard_rows, block_of_slot, window):
    total_blocks = block_of_slot.shape[0]
    block_len = shard_rows.shape[1]
    catalog = jnp.arange(total_blocks)
    home_row = jnp.sum(
        jnp.where(block_of_slot[None, :] == catalog[:, None], catalog[None, :], 0), axis=1
    )
    first_block = jnp.clip((attach_slots - window) // block_len, 0, total_blocks - 1)
    second_block = jnp.clip(first_block + 1, 0, total_blocks - 1)
    offset = attach_slots - window - first_block * block_len
    pair = jnp.stack([home_row[first_block], home_row[second_block]], axis=1)
    both = shard_rows[pair].reshape(attach_slots.shape[0], 2 * block_len, -1)
    picks = (
        jnp.arange(2 * block_len)[None, None, :]
        == offset[:, None, None] + jnp.arange(window)[None, :, None]
    ).astype(jnp.bfloat16)
    return jnp.einsum(
        "ruk,rkd->rud", picks, both, preferred_element_type=jnp.float32
    ).astype(jnp.bfloat16)


def local(
    suffix_tokens,
    route_lengths,
    dest_perm,
    attach_points,
    prefix_cache,
    block_of_slot,
    sink_logits,
    attn_gain,
    w_query,
    w_keyval,
    w_out,
    mlp_gain,
    w_gate,
    w_up,
    w_down,
):
    peers = lax.axis_size("req")
    splits = lax.axis_size("tp")
    request_index = lax.axis_index("req")
    tensor_index = lax.axis_index("tp")
    slot_count, slot_length, features = suffix_tokens.shape
    feature_share = features // splits
    value_heads = w_keyval.shape[1]
    head_dim = w_keyval.shape[2] // 2
    peer_ids = jnp.arange(peers)
    slot_steps = jnp.arange(slot_length)
    my_row = lax.dynamic_index_in_dim(dest_perm, request_index, 0, keepdims=False)
    attach_table = attach_points.reshape(peers, peers)
    arriving_lengths = lax.dynamic_index_in_dim(route_lengths, request_index, 0, keepdims=False)
    arriving = (dest_perm == request_index).astype(jnp.int32)
    arriving_attach = jnp.sum(attach_table * arriving, axis=1)
    send_order = jnp.sum(
        jnp.where(my_row[None, :] == peer_ids[:, None], peer_ids[None, :], 0), axis=1
    )
    run_ends = jnp.cumsum(arriving_lengths)
    starts = run_ends - arriving_lengths
    packed_ids = jnp.arange(CAP)
    source_of = jnp.sum((run_ends[None, :] <= packed_ids[:, None]).astype(jnp.int32), axis=1)
    source_hot = (source_of[:, None] == peer_ids[None, :]).astype(jnp.int32)
    token_index = packed_ids - jnp.sum(source_hot * starts[None, :], axis=1)
    positions = jnp.sum(source_hot * arriving_attach[None, :], axis=1) + token_index
    flat_index = source_of * slot_length + token_index
    slot_source = jnp.clip(starts[:, None] + slot_steps[None, :], 0, CAP - 1).reshape(-1)
    live_mask = slot_steps[None, :] < arriving_lengths[:, None]

    slot_pick = (
        (jnp.arange(CAP)[None, :] == slot_source[:, None]) & live_mask.reshape(-1)[:, None]
    ).astype(jnp.bfloat16)
    pack_pick = (
        jnp.arange(peers * slot_length)[None, :] == flat_index[:, None]
    ).astype(jnp.bfloat16)

    def to_slots(values):
        moved = jnp.dot(slot_pick, values, preferred_element_type=jnp.float32)
        return moved.astype(values.dtype).reshape((peers, slot_length) + values.shape[1:])

    def to_packed(values):
        return jnp.dot(pack_pick, values, preferred_element_type=jnp.float32).astype(values.dtype)

    my_features = lax.dynamic_slice_in_dim(
        suffix_tokens, tensor_index * feature_share, feature_share, 2
    )
    send_pick = (send_order[:, None] == peer_ids[None, :]).astype(jnp.bfloat16)
    outgoing = jnp.einsum(
        "dk,ktf->dtf", send_pick, my_features, preferred_element_type=jnp.float32
    ).astype(jnp.bfloat16)
    landed = lax.all_to_all(outgoing, "req", split_axis=0, concat_axis=0, tiled=True)
    input_part = to_packed(landed.reshape(peers * slot_length, feature_share))
    held_here, block_len = prefix_cache.shape[0], prefix_cache.shape[1]
    spread = jnp.broadcast_to(
        prefix_cache.reshape((1, held_here, block_len, -1)),
        (peers, held_here, block_len, prefix_cache.shape[2] * prefix_cache.shape[3]),
    )
    spread, input_part = lax.optimization_barrier((spread, input_part))
    prefix_rows = lax.all_to_all(spread, "req", split_axis=0, concat_axis=0, tiled=True)
    tail_rows = fetch_prefix(
        arriving_attach,
        prefix_rows.reshape((peers * held_here, block_len, -1)),
        block_of_slot,
        WINDOW,
    )
    input_rows = lax.all_gather(input_part, "tp", axis=1, tiled=True)
    row_total = input_part.shape[0]
    normed_in = norm_rows(input_rows, attn_gain)
    queries = jnp.dot(normed_in, w_query, preferred_element_type=jnp.float32).reshape(
        row_total, -1, head_dim
    )
    queries = rotate(queries, positions).astype(jnp.bfloat16)
    paired = jnp.dot(
        normed_in, w_keyval.reshape(features, -1), preferred_element_type=jnp.float32
    ).reshape(row_total, value_heads, 2 * head_dim)
    rotated = rotate(paired[..., :head_dim], positions)
    paired = jnp.concatenate([rotated, paired[..., head_dim:]], axis=-1).astype(jnp.bfloat16)
    attended = attend_pallas(
        to_slots(queries.reshape(row_total, -1)),
        to_slots(paired.reshape(row_total, -1)),
        tail_rows,
        sink_logits,
    ).reshape(peers * slot_length, -1)
    attended = to_packed(attended)
    partial_value = jnp.dot(attended, w_out, preferred_element_type=jnp.float32)
    summed = lax.psum_scatter(
        partial_value.astype(jnp.bfloat16), "tp", scatter_dimension=1, tiled=True
    ).astype(jnp.float32)
    residual_part = (input_part.astype(jnp.float32) + summed).astype(jnp.bfloat16)
    residual = lax.all_gather(residual_part, "tp", axis=1, tiled=True)
    normed_mid = norm_rows(residual, mlp_gain)
    gate_proj = jnp.dot(normed_mid, w_gate, preferred_element_type=jnp.float32)
    up_proj = jnp.dot(normed_mid, w_up, preferred_element_type=jnp.float32)
    hidden = (jax.nn.silu(gate_proj) * up_proj).astype(jnp.bfloat16)
    down_sum = lax.psum_scatter(
        jnp.dot(hidden, w_down, preferred_element_type=jnp.float32).astype(jnp.bfloat16),
        "tp",
        scatter_dimension=1,
        tiled=True,
    ).astype(jnp.float32)
    out_rows = (residual_part.astype(jnp.float32) + down_sum).astype(jnp.bfloat16)
    out_slots = to_slots(out_rows)
    returned = lax.all_to_all(out_slots, "req", split_axis=0, concat_axis=0, tiled=True)
    return_pick = (my_row[:, None] == peer_ids[None, :]).astype(jnp.bfloat16)
    return jnp.einsum(
        "kd,dtf->ktf", return_pick, returned, preferred_element_type=jnp.float32
    ).astype(jnp.bfloat16)


def solution(mesh):
    in_specs = (
        P("req", None, None),
        P(),
        P(),
        P(),
        P("req", None, "tp", None),
        P(),
        P("tp"),
        P(),
        P(None, "tp"),
        P(None, "tp", None),
        P("tp", None),
        P(),
        P(None, "tp"),
        P(None, "tp"),
        P("tp", None),
    )
    out_specs = P("req", None, "tp")
    return jax.shard_map(local, mesh=mesh, in_specs=in_specs, out_specs=out_specs, check_vma=False)
```

```python
import jax
import jax.numpy as jnp
from jax import lax
from jax.sharding import PartitionSpec as P
from jax.experimental import pallas as pl
from jax.experimental.pallas import tpu as pltpu

WINDOW = 128
CAP = 768


ROPE_BASE = 150000.0
EPSILON = 1e-05


def norm_rows(inputs, gains):
    widened = inputs.astype(jnp.float32)
    factor = lax.rsqrt(jnp.mean(widened * widened, axis=-1, keepdims=True) + EPSILON)
    return (widened * factor * gains.astype(jnp.float32)).astype(jnp.bfloat16)


def rotate(vectors, positions):
    half_dim = vectors.shape[-1] // 2
    frequency = ROPE_BASE ** (-(jnp.arange(half_dim).astype(jnp.float32) * 2.0 / vectors.shape[-1]))
    angles = positions.astype(jnp.float32)[:, None, None] * frequency
    cosine = jnp.cos(angles)
    sine_part = jnp.sin(angles)
    first_half = vectors[..., :half_dim]
    second = vectors[..., half_dim:]
    return jnp.concatenate(
        [first_half * cosine - second * sine_part, second * cosine + first_half * sine_part],
        axis=-1,
    )


def attend(query_slots, paired_slots, tail_rows, sink_logits):
    peers, slot_length = (query_slots.shape[0], query_slots.shape[1])
    value_heads = paired_slots.shape[2]
    head_dim = paired_slots.shape[3] // 2
    group_size = query_slots.shape[2] // value_heads
    window = tail_rows.shape[1]
    grouped_query = query_slots.reshape(peers, slot_length, value_heads, group_size, head_dim)
    near_keys = jnp.concatenate([tail_rows, paired_slots], axis=1)
    score_scale = head_dim ** (-0.5)
    near_scores = (
        jnp.einsum(
            "ntkgd,nskd->nkgts",
            grouped_query,
            near_keys[..., :head_dim],
            preferred_element_type=jnp.float32,
        )
        * score_scale
    )
    sink_scores = sink_logits.reshape(value_heads, group_size)[None, :, :, None, None]
    slot_steps = jnp.arange(slot_length)
    columns = jnp.arange(window + slot_length)
    allowed = jnp.where(
        columns[None, :] < window,
        columns[None, :] > slot_steps[:, None],
        columns[None, :] - window <= slot_steps[:, None],
    )
    near_scores = jnp.where(allowed, near_scores, -jnp.inf)
    largest = jnp.maximum(jnp.max(near_scores, axis=-1, keepdims=True), sink_scores)
    near_weights = jnp.exp(near_scores - largest)
    normalizer = jnp.sum(near_weights, axis=-1, keepdims=True) + jnp.exp(sink_scores - largest)
    near_weights = (near_weights / normalizer).astype(jnp.bfloat16)
    mixed = jnp.einsum(
        "nkgts,nskd->ntkgd",
        near_weights,
        near_keys[..., head_dim:],
        preferred_element_type=jnp.float32,
    )
    return mixed.astype(jnp.bfloat16).reshape(
        peers * slot_length, value_heads * group_size * head_dim
    )


def attend_kernel(sink_ref, q_ref, kv_ref, tail_ref, o_ref):
    batch, slot_length = q_ref.shape[0], q_ref.shape[1]
    window = tail_ref.shape[1]
    head_dim = kv_ref.shape[2] // 2
    heads = q_ref.shape[2] // head_dim
    scale = head_dim ** (-0.5)
    step = lax.broadcasted_iota(jnp.int32, (slot_length, window), 0)
    column = lax.broadcasted_iota(jnp.int32, (slot_length, window), 1)
    tail_allowed = jnp.concatenate([column > step] * heads, axis=0)
    own_step = lax.broadcasted_iota(jnp.int32, (slot_length, slot_length), 0)
    own_column = lax.broadcasted_iota(jnp.int32, (slot_length, slot_length), 1)
    own_allowed = jnp.concatenate([own_column <= own_step] * heads, axis=0)
    sink = jnp.concatenate(
        [jnp.full((slot_length, 1), sink_ref[head], jnp.float32) for head in range(heads)],
        axis=0,
    )
    contract = (((1,), (1,)), ((), ()))
    for item in range(batch):
        kv = kv_ref[item]
        tail = tail_ref[item]
        query = q_ref[item]
        stacked = jnp.concatenate(
            [query[:, head * head_dim:(head + 1) * head_dim] for head in range(heads)], axis=0
        )
        tail_scores = lax.dot_general(
            stacked, tail[:, :head_dim], contract, preferred_element_type=jnp.float32
        ) * scale
        own_scores = lax.dot_general(
            stacked, kv[:, :head_dim], contract, preferred_element_type=jnp.float32
        ) * scale
        tail_scores = jnp.where(tail_allowed, tail_scores, -jnp.inf)
        own_scores = jnp.where(own_allowed, own_scores, -jnp.inf)
        largest = jnp.maximum(
            jnp.maximum(
                jnp.max(tail_scores, axis=1, keepdims=True),
                jnp.max(own_scores, axis=1, keepdims=True),
            ),
            sink,
        )
        tail_weights = jnp.exp(tail_scores - largest)
        own_weights = jnp.exp(own_scores - largest)
        normalizer = (
            jnp.sum(tail_weights, axis=1, keepdims=True)
            + jnp.sum(own_weights, axis=1, keepdims=True)
            + jnp.exp(sink - largest)
        )
        inverse = 1.0 / normalizer
        tail_weights = (tail_weights * inverse).astype(jnp.bfloat16)
        own_weights = (own_weights * inverse).astype(jnp.bfloat16)
        mixed = jnp.dot(
            tail_weights, tail[:, head_dim:], preferred_element_type=jnp.float32
        ) + jnp.dot(own_weights, kv[:, head_dim:], preferred_element_type=jnp.float32)
        mixed = mixed.astype(o_ref.dtype)
        for head in range(heads):
            o_ref[item, :, head * head_dim:(head + 1) * head_dim] = mixed[
                head * slot_length:(head + 1) * slot_length
            ]


def attend_pallas(joined_slots, width, tail_rows, sink_logits, batch=2):
    peers, slot_length, joined = joined_slots.shape
    window = tail_rows.shape[1]
    pair_width = joined - width
    head_dim = pair_width // 2
    heads = width // head_dim
    flops = peers * heads * 4 * slot_length * (window + slot_length) * head_dim
    moved = 2 * (joined_slots.size + peers * slot_length * width + tail_rows.size)
    return pl.pallas_call(
        attend_kernel,
        grid=(peers // batch,),
        in_specs=[
            pl.BlockSpec(memory_space=pltpu.SMEM),
            pl.BlockSpec((batch, slot_length, width), lambda n: (n, 0, 0)),
            pl.BlockSpec((batch, slot_length, pair_width), lambda n: (n, 0, width // pair_width)),
            pl.BlockSpec((batch, window, pair_width), lambda n: (n, 0, 0)),
        ],
        out_specs=pl.BlockSpec((batch, slot_length, width), lambda n: (n, 0, 0)),
        out_shape=jax.ShapeDtypeStruct((peers, slot_length, width), jnp.bfloat16),
        cost_estimate=pl.CostEstimate(
            flops=flops,
            transcendentals=peers * heads * slot_length * (window + slot_length),
            bytes_accessed=moved,
        ),
    )(sink_logits.astype(jnp.float32), joined_slots, joined_slots, tail_rows)


def fetch_prefix(attach_slots, shard_rows, block_of_slot, window):
    total_blocks = block_of_slot.shape[0]
    block_len = shard_rows.shape[1]
    catalog = jnp.arange(total_blocks)
    home_row = jnp.sum(
        jnp.where(block_of_slot[None, :] == catalog[:, None], catalog[None, :], 0), axis=1
    )
    first_block = jnp.clip((attach_slots - window) // block_len, 0, total_blocks - 1)
    second_block = jnp.clip(first_block + 1, 0, total_blocks - 1)
    offset = attach_slots - window - first_block * block_len
    pair = jnp.stack([home_row[first_block], home_row[second_block]], axis=1)
    both = shard_rows[pair].reshape(attach_slots.shape[0], 2 * block_len, -1)
    picks = (
        jnp.arange(2 * block_len)[None, None, :]
        == offset[:, None, None] + jnp.arange(window)[None, :, None]
    ).astype(jnp.bfloat16)
    return jnp.einsum(
        "ruk,rkd->rud", picks, both, preferred_element_type=jnp.float32
    ).astype(jnp.bfloat16)


def local(
    suffix_tokens,
    route_lengths,
    dest_perm,
    attach_points,
    prefix_cache,
    block_of_slot,
    sink_logits,
    attn_gain,
    w_query,
    w_keyval,
    w_out,
    mlp_gain,
    w_gate,
    w_up,
    w_down,
):
    peers = lax.axis_size("req")
    splits = lax.axis_size("tp")
    request_index = lax.axis_index("req")
    tensor_index = lax.axis_index("tp")
    slot_count, slot_length, features = suffix_tokens.shape
    feature_share = features // splits
    value_heads = w_keyval.shape[1]
    head_dim = w_keyval.shape[2] // 2
    peer_ids = jnp.arange(peers)
    slot_steps = jnp.arange(slot_length)
    my_row = lax.dynamic_index_in_dim(dest_perm, request_index, 0, keepdims=False)
    attach_table = attach_points.reshape(peers, peers)
    arriving_lengths = lax.dynamic_index_in_dim(route_lengths, request_index, 0, keepdims=False)
    arriving = (dest_perm == request_index).astype(jnp.int32)
    arriving_attach = jnp.sum(attach_table * arriving, axis=1)
    send_order = jnp.sum(
        jnp.where(my_row[None, :] == peer_ids[:, None], peer_ids[None, :], 0), axis=1
    )
    run_ends = jnp.cumsum(arriving_lengths)
    starts = run_ends - arriving_lengths
    packed_ids = jnp.arange(CAP)
    source_of = jnp.sum((run_ends[None, :] <= packed_ids[:, None]).astype(jnp.int32), axis=1)
    source_hot = (source_of[:, None] == peer_ids[None, :]).astype(jnp.int32)
    token_index = packed_ids - jnp.sum(source_hot * starts[None, :], axis=1)
    positions = jnp.sum(source_hot * arriving_attach[None, :], axis=1) + token_index
    flat_index = source_of * slot_length + token_index
    slot_source = jnp.clip(starts[:, None] + slot_steps[None, :], 0, CAP - 1).reshape(-1)
    live_mask = slot_steps[None, :] < arriving_lengths[:, None]

    slot_pick = (
        (jnp.arange(CAP)[None, :] == slot_source[:, None]) & live_mask.reshape(-1)[:, None]
    ).astype(jnp.bfloat16)
    pack_pick = (
        jnp.arange(peers * slot_length)[None, :] == flat_index[:, None]
    ).astype(jnp.bfloat16)

    def to_slots(values):
        moved = jnp.dot(slot_pick, values, preferred_element_type=jnp.float32)
        return moved.astype(values.dtype).reshape((peers, slot_length) + values.shape[1:])

    def to_packed(values):
        return jnp.dot(pack_pick, values, preferred_element_type=jnp.float32).astype(values.dtype)

    my_features = lax.dynamic_slice_in_dim(
        suffix_tokens, tensor_index * feature_share, feature_share, 2
    )
    send_pick = (send_order[:, None] == peer_ids[None, :]).astype(jnp.bfloat16)
    outgoing = jnp.einsum(
        "dk,ktf->dtf", send_pick, my_features, preferred_element_type=jnp.float32
    ).astype(jnp.bfloat16)
    landed = lax.all_to_all(outgoing, "req", split_axis=0, concat_axis=0, tiled=True)
    input_part = to_packed(landed.reshape(peers * slot_length, feature_share))
    held_here, block_len = prefix_cache.shape[0], prefix_cache.shape[1]
    spread = jnp.broadcast_to(
        prefix_cache.reshape((1, held_here, block_len, -1)),
        (peers, held_here, block_len, prefix_cache.shape[2] * prefix_cache.shape[3]),
    )
    spread, input_part = lax.optimization_barrier((spread, input_part))
    prefix_rows = lax.all_to_all(spread, "req", split_axis=0, concat_axis=0, tiled=True)
    tail_rows = fetch_prefix(
        arriving_attach,
        prefix_rows.reshape((peers * held_here, block_len, -1)),
        block_of_slot,
        WINDOW,
    )
    input_rows = lax.all_gather(input_part, "tp", axis=1, tiled=True)
    row_total = input_part.shape[0]
    normed_in = norm_rows(input_rows, attn_gain)
    queries = jnp.dot(normed_in, w_query, preferred_element_type=jnp.float32).reshape(
        row_total, -1, head_dim
    )
    queries = rotate(queries, positions).astype(jnp.bfloat16)
    paired = jnp.dot(
        normed_in, w_keyval.reshape(features, -1), preferred_element_type=jnp.float32
    ).reshape(row_total, value_heads, 2 * head_dim)
    rotated = rotate(paired[..., :head_dim], positions)
    paired = jnp.concatenate([rotated, paired[..., head_dim:]], axis=-1).astype(jnp.bfloat16)
    attended = attend_pallas(
        to_slots(
            jnp.concatenate(
                [queries.reshape(row_total, -1), paired.reshape(row_total, -1)], axis=1
            )
        ),
        queries.shape[1] * queries.shape[2],
        tail_rows,
        sink_logits,
    ).reshape(peers * slot_length, -1)
    attended = to_packed(attended)
    partial_value = jnp.dot(attended, w_out, preferred_element_type=jnp.float32)
    summed = lax.psum_scatter(
        partial_value.astype(jnp.bfloat16), "tp", scatter_dimension=1, tiled=True
    ).astype(jnp.float32)
    residual_part = (input_part.astype(jnp.float32) + summed).astype(jnp.bfloat16)
    residual = lax.all_gather(residual_part, "tp", axis=1, tiled=True)
    normed_mid = norm_rows(residual, mlp_gain)
    gate_proj = jnp.dot(normed_mid, w_gate, preferred_element_type=jnp.float32)
    up_proj = jnp.dot(normed_mid, w_up, preferred_element_type=jnp.float32)
    hidden = (jax.nn.silu(gate_proj) * up_proj).astype(jnp.bfloat16)
    down_sum = lax.psum_scatter(
        jnp.dot(hidden, w_down, preferred_element_type=jnp.float32).astype(jnp.bfloat16),
        "tp",
        scatter_dimension=1,
        tiled=True,
    ).astype(jnp.float32)
    out_rows = (residual_part.astype(jnp.float32) + down_sum).astype(jnp.bfloat16)
    out_slots = to_slots(out_rows)
    returned = lax.all_to_all(out_slots, "req", split_axis=0, concat_axis=0, tiled=True)
    return_pick = (my_row[:, None] == peer_ids[None, :]).astype(jnp.bfloat16)
    return jnp.einsum(
        "kd,dtf->ktf", return_pick, returned, preferred_element_type=jnp.float32
    ).astype(jnp.bfloat16)


def solution(mesh):
    in_specs = (
        P("req", None, None),
        P(),
        P(),
        P(),
        P("req", None, "tp", None),
        P(),
        P("tp"),
        P(),
        P(None, "tp"),
        P(None, "tp", None),
        P("tp", None),
        P(),
        P(None, "tp"),
        P(None, "tp"),
        P("tp", None),
    )
    out_specs = P("req", None, "tp")
    return jax.shard_map(local, mesh=mesh, in_specs=in_specs, out_specs=out_specs, check_vma=False)
```
